128 devices in a mesh: skyy: 8 (over x, core), skyx: 16 (over z, y).
Axes of the slice: x: 4, y: 4, z: 4, core: 2. Of those that a mesh axis runs over, the one named last changes fastest.
Arguments:
- tiles: bfloat16 [8, 128, 256, 256], P('skyy', 'skyx'), may hold values from -6 to 6
- coeffs: bfloat16 [8, 128, 5, 256, 256], P('skyy', 'skyx'), may hold values from -4 to 4
- weights: bfloat16 [8, 128], P('skyy', 'skyx'), may hold values from 0.25 to 4
- tile_slot: int32 [8, 128], P('skyy', 'skyx'), may hold values from 0 to 31, as said below
- slot_offset: int32 [2, 8, 512], P(None, 'skyy', 'skyx'), may hold values from -224 to 480
Outputs:
- coadd: float32 [4096, 8192], P('skyy', 'skyx')
- detection: float32 [4096, 8192], P('skyy', 'skyx')
The draws below stay inside these ranges and needn't reach their ends.
Inputs may be any that keep to these rules, and one draw needn't show every extreme that they name: `tile_slot`: within one device the values are distinct; each device sends at most 2 tiles to one patch, and in every row of patches one patch receives 2 tiles from every device of that row.
All inputs are finite; a program needn't handle non-finite values.
Results may differ from the reference program's by a relative error of at most 0.013.
Values may be sent and summed in bfloat16 or wider, within the bound.
No kernel may reach another device: no remote copies, remote signals or barrier semaphores. Data moves between devices by JAX's collectives and lax.ppermute only.
A program may use at most 192 MiB of HBM per device.

```python
import math
import jax
import jax.numpy as jnp
from jax import lax

TILE = 256
NB = 5
REACH = 10
CAP = 2
PATCH = 512
V_DEV = 8
SLOTS = 32
N_SKYY = 8
N_SKYX = 16


def draw_tile_slot(key, part):
    slots = N_SKYX * CAP
    hot = jax.random.randint(jax.random.fold_in(key, 7), (N_SKYY,), 0, N_SKYX)
    scores = jax.random.randint(jax.random.fold_in(key, 11), (N_SKYY, N_SKYX, slots), 0, 1 << 20)
    index = jnp.arange(slots, dtype=jnp.int32)
    scores = scores * slots + index[None, None, :]
    is_hot = index[None, None, :] // CAP == hot[:, None, None]
    scores = jnp.where(is_hot, -1 - index[None, None, :], scores)
    order = jnp.argsort(scores, axis=-1, stable=True)
    return order[:, :, :V_DEV].reshape(N_SKYY, N_SKYX * V_DEV).astype(jnp.int32)


def set_ends(values, stream_key, least, top_value):
    index_at = [jax.random.randint(jax.random.fold_in(stream_key, axis), (), 0, length) for axis, length in enumerate(values.shape)]
    main_axis = values.shape.index(max(values.shape))
    neighbour = index_at[:main_axis] + [(index_at[main_axis] + 1) % values.shape[main_axis]] + index_at[main_axis + 1:]
    return values.at[tuple(index_at)].set(least).at[tuple(neighbour)].set(top_value)


def shard_levels(rng, shape, shards, smallest, high):
    loudness = 1.0
    for dim, parts in shards:
        heights = jax.random.uniform(jax.random.fold_in(jax.random.fold_in(rng, 6), dim), (parts,), jnp.float32, smallest / len(shards), high / len(shards))
        loudness = loudness * jnp.repeat(jnp.exp(heights), shape[dim] // parts).reshape((-1,) + (1,) * (len(shape) - 1 - dim))
    return loudness


def bell_draw(rng, shape, scale, most, split=(), held_as=jnp.bfloat16):
    loudness = shard_levels(rng, shape, split, -0.22, 0.18) if split else 1.0
    entries = jax.random.normal(rng, shape, jnp.float32) * scale * loudness
    return jnp.minimum(jnp.maximum(entries, -most), most).astype(held_as)


def setup_inputs(seed: int = 0) -> dict:
    key_list = jax.random.split(jax.random.key(seed), 6)
    return {
        "tiles": bell_draw(key_list[0], (N_SKYY, N_SKYX * V_DEV, TILE, TILE), 1.0, 6.0, ((0, 8), (1, 16))),
        "coeffs": bell_draw(key_list[1], (N_SKYY, N_SKYX * V_DEV, NB, TILE, TILE), 0.6, 4.0, ((0, 8), (1, 16))),
        "weights": jnp.clip(jnp.exp(math.log(4.0) - 2.7725887 * jax.random.uniform(key_list[2], (N_SKYY, N_SKYX * V_DEV), jnp.float32) ** shard_levels(key_list[2], (N_SKYY, N_SKYX * V_DEV), ((0, 8), (1, 16)), -0.2, 0.2)), 0.25, 4.0).astype(jnp.bfloat16),
        "tile_slot": draw_tile_slot(jax.random.fold_in(key_list[5], 71), 0),
        "slot_offset": set_ends(jax.random.randint(key_list[4], (2, N_SKYY, N_SKYX * SLOTS), -(TILE - TILE // 8), PATCH - TILE // 8 + 1), jax.random.fold_in(key_list[4], 1), -(TILE - TILE // 8), (PATCH - TILE // 8 + 1) - 1).astype(jnp.int32),
    }


basis_widths = (1.0, 1.8, 2.6, 3.6, 5.0)
detect_width = 2.5


def band_matrices(size):
    rows = jnp.arange(size, dtype=jnp.int32)[:, None]
    cols = jnp.arange(size, dtype=jnp.int32)[None, :]
    gap = (cols - rows).astype(jnp.float32)
    inside = jnp.abs(cols - rows) <= REACH
    taps = jnp.arange(-REACH, REACH + 1).astype(jnp.float32)
    mats = []
    for width in basis_widths:
        total = jnp.sum(jnp.exp(-taps * taps / (2.0 * width * width)))
        mats.append(jnp.where(inside, jnp.exp(-gap * gap / (2.0 * width * width)) / total, 0.0))
    return jnp.stack(mats).astype(jnp.bfloat16)


def match_tile(tile, coeff, basis):
    high = lax.Precision.HIGHEST
    vert = jnp.einsum('bij,jk->bik', basis.astype(jnp.float32), tile.astype(jnp.float32), precision=high).astype(jnp.bfloat16)
    horiz = jnp.einsum('bik,bjk->bij', vert.astype(jnp.float32), basis.astype(jnp.float32), precision=high)
    result = jnp.sum(coeff.astype(jnp.float32) * horiz, axis=0).astype(jnp.bfloat16)
    return lax.optimization_barrier(result)


def coadd_patch(matched, slot_weight, offsets):
    size = matched.shape[1]
    canvas = PATCH + 2 * size
    zero_canvas = jnp.zeros((canvas, canvas), jnp.float32)

    def add_one(index, carry):
        numer, cover = carry
        row = offsets[0, index] + size
        col = offsets[1, index] + size
        weight = slot_weight[index].astype(jnp.float32)
        region = lax.dynamic_slice(numer, (row, col), (size, size))
        numer = lax.dynamic_update_slice(numer, region + weight * matched[index].astype(jnp.float32), (row, col))
        footprint = lax.dynamic_slice(cover, (row, col), (size, size))
        cover = lax.dynamic_update_slice(cover, footprint + weight, (row, col))
        return numer, cover

    numer, cover = lax.fori_loop(0, matched.shape[0], add_one, (zero_canvas, zero_canvas))
    numer = numer[size:size + PATCH, size:size + PATCH]
    cover = cover[size:size + PATCH, size:size + PATCH]
    return numer / (1.0 + cover)


def detect(extended, out_rows, out_cols):
    taps = jnp.arange(-REACH, REACH + 1).astype(jnp.float32)
    kernel = jnp.exp(-taps * taps / (2.0 * detect_width * detect_width))
    kernel = kernel / jnp.sum(kernel)
    vert = jnp.zeros((out_rows, extended.shape[1]), jnp.float32)
    for step in range(2 * REACH + 1):
        vert = vert + kernel[step] * extended[step:step + out_rows, :]
    result = jnp.zeros((out_rows, out_cols), jnp.float32)
    for step in range(2 * REACH + 1):
        result = result + kernel[step] * vert[:, step:step + out_cols]
    return result


def reference(tiles, coeffs, weights, tile_slot, slot_offset):
    slots = N_SKYX * CAP
    basis = band_matrices(TILE)
    patch_rows = []
    for sky_row in range(N_SKYY):
        matched = lax.map(lambda pair: match_tile(pair[0], pair[1], basis), (tiles[sky_row], coeffs[sky_row]))
        owner_slot = tile_slot[sky_row].reshape(N_SKYX, V_DEV)
        hits = owner_slot[:, :, None] == jnp.arange(slots, dtype=jnp.int32)[None, None, :]
        present = jnp.any(hits, axis=1)
        which = jnp.sum(jnp.where(hits, jnp.arange(V_DEV, dtype=jnp.int32)[None, :, None], 0), axis=1).astype(jnp.int32)
        source = (jnp.arange(N_SKYX, dtype=jnp.int32)[:, None] * V_DEV + which).astype(jnp.int32)
        row_weight = weights[sky_row]
        row_offsets = slot_offset[:, sky_row, :]

        def one_patch(column):
            start = (column * CAP).astype(jnp.int32)
            pick = lax.dynamic_slice_in_dim(source, start, CAP, 1).reshape(-1)
            live = lax.dynamic_slice_in_dim(present, start, CAP, 1).reshape(-1)
            slot_tiles = matched[pick]
            slot_weight = jnp.where(live, row_weight[pick], jnp.zeros((), jnp.bfloat16))
            offsets = lax.dynamic_slice_in_dim(row_offsets, (column * slots).astype(jnp.int32), slots, 1)
            return coadd_patch(slot_tiles, slot_weight, offsets)

        patch_rows.append(lax.map(one_patch, jnp.arange(N_SKYX, dtype=jnp.int32)))
    patches = jnp.stack(patch_rows)
    coadd = patches.transpose(0, 2, 1, 3).reshape(N_SKYY * PATCH, N_SKYX * PATCH)
    padded = jnp.pad(coadd, REACH)
    detection = detect(padded, coadd.shape[0], coadd.shape[1])
    return coadd, detection
```

```python
import numpy as np
import jax
import jax.numpy as jnp
from jax import lax
from jax.sharding import PartitionSpec as P

NB = 5
REACH = 10
CAP = 2
PATCH = 512


basis_widths = (1.0, 1.8, 2.6, 3.6, 5.0)
detect_width = 2.5


def band_matrices(size):
    rows = np.arange(size, dtype=np.int32)[:, None]
    cols = np.arange(size, dtype=np.int32)[None, :]
    gap = (cols - rows).astype(np.float32)
    inside = np.abs(cols - rows) <= REACH
    taps = np.arange(-REACH, REACH + 1).astype(np.float32)
    mats = []
    for width in basis_widths:
        scale = np.float32(2.0 * width * width)
        total = np.sum(np.exp(-taps * taps / scale), dtype=np.float32)
        mats.append(np.where(inside, np.exp(-gap * gap / scale) / total, np.float32(0.0)))
    return np.stack(mats).astype(np.float32).astype(jnp.bfloat16)


def detect_band(out_size, in_size):
    taps = jnp.arange(-REACH, REACH + 1).astype(jnp.float32)
    kernel = jnp.exp(-taps * taps / (2.0 * detect_width * detect_width))
    kernel = kernel / jnp.sum(kernel)
    rows = jnp.arange(out_size, dtype=jnp.int32)[:, None]
    cols = jnp.arange(in_size, dtype=jnp.int32)[None, :]
    gap = cols - rows
    inside = (gap >= 0) & (gap <= 2 * REACH)
    return jnp.where(inside, kernel[jnp.clip(gap, 0, 2 * REACH)], 0.0)


def match_all(tiles, coeffs, basis):
    vert = jnp.einsum(
        "bij,mjk->mbik", basis, tiles, preferred_element_type=jnp.float32
    ).astype(jnp.bfloat16)
    horiz = jnp.einsum("mbik,bjk->mbij", vert, basis, preferred_element_type=jnp.float32)
    return jnp.sum(coeffs.astype(jnp.float32) * horiz, axis=1).astype(jnp.bfloat16)


def coadd_patch(matched, slot_weight, offsets, patch):
    slot_count = matched.shape[0]
    size = matched.shape[1]
    local = jnp.arange(size, dtype=jnp.int32)
    pixel = jnp.arange(patch, dtype=jnp.int32)
    row_hit = offsets[0][:, None, None] + local[None, :, None] == pixel[None, None, :]
    col_hit = offsets[1][:, None, None] + local[None, :, None] == pixel[None, None, :]
    row_place = row_hit.astype(jnp.bfloat16)
    placed = jnp.einsum("sip,sij->psj", row_place, matched, preferred_element_type=jnp.float32)
    placed = placed.astype(jnp.bfloat16).reshape(patch, slot_count * size)
    zero_weight = jnp.zeros((), jnp.bfloat16)
    col_place = jnp.where(col_hit, slot_weight[:, None, None], zero_weight).reshape(
        slot_count * size, patch
    )
    numer = jnp.dot(placed, col_place, preferred_element_type=jnp.float32)
    row_cover = jnp.any(row_hit, axis=1).astype(jnp.float32)
    col_cover = jnp.where(jnp.any(col_hit, axis=1), slot_weight[:, None].astype(jnp.float32), 0.0)
    cover = jnp.dot(
        row_cover.T, col_cover, precision=lax.Precision.HIGHEST, preferred_element_type=jnp.float32
    )
    return numer / (1.0 + cover)


def halo_extend(coadd):
    ny = lax.axis_size("skyy")
    nx = lax.axis_size("skyx")
    r = REACH
    both = ("skyy", "skyx")

    def flat(a, b):
        return a * nx + b

    down = [(i, i + 1) for i in range(ny - 1)]
    up = [(i + 1, i) for i in range(ny - 1)]
    right = [(j, j + 1) for j in range(nx - 1)]
    left = [(j + 1, j) for j in range(nx - 1)]
    top = lax.ppermute(coadd[-r:, :], "skyy", down)
    bottom = lax.ppermute(coadd[:r, :], "skyy", up)
    west = lax.ppermute(coadd[:, -r:], "skyx", right)
    east = lax.ppermute(coadd[:, :r], "skyx", left)
    tl = lax.ppermute(
        coadd[-r:, -r:], both,
        [(flat(a, b), flat(a + 1, b + 1)) for a in range(ny - 1) for b in range(nx - 1)],
    )
    tr = lax.ppermute(
        coadd[-r:, :r], both,
        [(flat(a, b + 1), flat(a + 1, b)) for a in range(ny - 1) for b in range(nx - 1)],
    )
    bl = lax.ppermute(
        coadd[:r, -r:], both,
        [(flat(a + 1, b), flat(a, b + 1)) for a in range(ny - 1) for b in range(nx - 1)],
    )
    br = lax.ppermute(
        coadd[:r, :r], both,
        [(flat(a + 1, b + 1), flat(a, b)) for a in range(ny - 1) for b in range(nx - 1)],
    )
    upper = jnp.concatenate([tl, top, tr], axis=1)
    middle = jnp.concatenate([west, coadd, east], axis=1)
    lower = jnp.concatenate([bl, bottom, br], axis=1)
    return jnp.concatenate([upper, middle, lower], axis=0)


def body(tiles, coeffs, weights, tile_slot, slot_offset):
    count = tiles.shape[1]
    size = tiles.shape[2]
    columns = lax.axis_size("skyx")
    slots = columns * CAP
    patch = PATCH
    basis = jnp.asarray(band_matrices(size))
    own_tiles = tiles[0]
    own_coeffs = coeffs[0]
    own_weight = weights[0]
    own_slot = tile_slot[0]
    offsets = slot_offset[:, 0, :]
    hits = own_slot[None, :] == jnp.arange(slots, dtype=jnp.int32)[:, None]
    present = jnp.any(hits, axis=1)
    which = jnp.sum(jnp.where(hits, jnp.arange(count, dtype=jnp.int32)[None, :], 0), axis=1)
    send_weight = jnp.where(present, own_weight[which], jnp.zeros((), jnp.bfloat16))
    send_weight = send_weight.reshape(columns, CAP)
    own_matched = match_all(own_tiles, own_coeffs, basis)
    send_matched = jnp.where(
        present[:, None, None], own_matched[which], jnp.zeros((), jnp.bfloat16)
    ).reshape(columns, CAP, size, size)
    matched, recv_weight = (
        lax.all_to_all(send_matched, "skyx", split_axis=0, concat_axis=0, tiled=True),
        lax.all_to_all(send_weight, "skyx", split_axis=0, concat_axis=0, tiled=True),
    )
    matched = matched.reshape(slots, size, size)
    recv_weight = recv_weight.reshape(slots)
    coadd = coadd_patch(matched, recv_weight, offsets, patch)
    extended = halo_extend(coadd)
    ext = patch + 2 * REACH
    band = detect_band(patch, ext)
    high = lax.Precision.HIGH
    vert = jnp.dot(band, extended, precision=high, preferred_element_type=jnp.float32)
    detection = jnp.dot(vert, band.T, precision=high, preferred_element_type=jnp.float32)
    return (coadd, detection)


def solution(mesh):
    in_specs = (
        P("skyy", "skyx", None, None),
        P("skyy", "skyx", None, None, None),
        P("skyy", "skyx"),
        P("skyy", "skyx"),
        P(None, "skyy", "skyx"),
    )
    out_specs = (P("skyy", "skyx"), P("skyy", "skyx"))
    return jax.shard_map(body, mesh=mesh, in_specs=in_specs, out_specs=out_specs, check_vma=False)
```

```python
import numpy as np
import jax
import jax.numpy as jnp
from jax import lax
from jax.sharding import PartitionSpec as P

NB = 5
REACH = 10
CAP = 2
PATCH = 512


basis_widths = (1.0, 1.8, 2.6, 3.6, 5.0)
detect_width = 2.5


def band_matrices(size):
    rows = np.arange(size, dtype=np.int32)[:, None]
    cols = np.arange(size, dtype=np.int32)[None, :]
    gap = (cols - rows).astype(np.float32)
    inside = np.abs(cols - rows) <= REACH
    taps = np.arange(-REACH, REACH + 1).astype(np.float32)
    mats = []
    for width in basis_widths:
        scale = np.float32(2.0 * width * width)
        total = np.sum(np.exp(-taps * taps / scale), dtype=np.float32)
        mats.append(np.where(inside, np.exp(-gap * gap / scale) / total, np.float32(0.0)))
    return np.stack(mats).astype(np.float32).astype(jnp.bfloat16)


def detect_band(out_size, in_size):
    taps = jnp.arange(-REACH, REACH + 1).astype(jnp.float32)
    kernel = jnp.exp(-taps * taps / (2.0 * detect_width * detect_width))
    kernel = kernel / jnp.sum(kernel)
    rows = jnp.arange(out_size, dtype=jnp.int32)[:, None]
    cols = jnp.arange(in_size, dtype=jnp.int32)[None, :]
    gap = cols - rows
    inside = (gap >= 0) & (gap <= 2 * REACH)
    return jnp.where(inside, kernel[jnp.clip(gap, 0, 2 * REACH)], 0.0)


def match_all(tiles, coeffs, basis):
    vert = jnp.einsum(
        "bij,mjk->mbik", basis, tiles, preferred_element_type=jnp.float32
    ).astype(jnp.bfloat16)
    horiz = jnp.einsum("mbik,bjk->mbij", vert, basis, preferred_element_type=jnp.float32)
    return jnp.sum(coeffs.astype(jnp.float32) * horiz, axis=1).astype(jnp.bfloat16)


def coadd_patch(matched, slot_weight, offsets, patch):
    slot_count = matched.shape[0]
    size = matched.shape[1]
    local = jnp.arange(size, dtype=jnp.int32)
    pixel = jnp.arange(patch, dtype=jnp.int32)
    col_hit = offsets[1][:, None, None] + local[None, :, None] == pixel[None, None, :]
    row_hit = offsets[0][None, :, None] + local[None, None, :] == pixel[:, None, None]
    col_place = col_hit.astype(jnp.bfloat16)
    shifted = jnp.einsum(
        "sij,sjq->siq", matched, col_place, preferred_element_type=jnp.float32
    ).astype(jnp.bfloat16)
    zero_weight = jnp.zeros((), jnp.bfloat16)
    row_place = jnp.where(row_hit, slot_weight[None, :, None], zero_weight)
    numer = jnp.dot(
        row_place.reshape(patch, slot_count * size),
        shifted.reshape(slot_count * size, patch),
        preferred_element_type=jnp.float32,
    )
    row_cover = jnp.where(jnp.any(row_hit, axis=2), slot_weight[None, :], zero_weight)
    col_cover = jnp.any(col_hit, axis=1).astype(jnp.bfloat16)
    cover = jnp.dot(row_cover, col_cover, preferred_element_type=jnp.float32)
    return numer / (1.0 + cover)


def split(x):
    hi = lax.reduce_precision(x, exponent_bits=8, mantissa_bits=7)
    return hi.astype(jnp.bfloat16), (x - hi).astype(jnp.bfloat16)


def mm3(a, b, dims=(((1,), (0,)), ((), ()))):
    ah, al = a
    bh, bl = b

    def one(x, y):
        return lax.dot_general(x, y, dims, preferred_element_type=jnp.float32)

    return one(ah, bh) + (one(al, bh) + one(ah, bl))


def detect(coadd):
    ny = lax.axis_size("skyy")
    nx = lax.axis_size("skyx")
    r = REACH
    patch = coadd.shape[0]
    band = detect_band(patch, patch + 2 * r)
    g_head = split(band[:, :r])
    g_mid = split(band[:, r:patch + r])
    g_tail = split(band[:, patch + r:])
    down = [(i, i + 1) for i in range(ny - 1)]
    up = [(i + 1, i) for i in range(ny - 1)]
    right = [(j, j + 1) for j in range(nx - 1)]
    left = [(j + 1, j) for j in range(nx - 1)]
    top = lax.ppermute(coadd[-r:, :], "skyy", down)
    bottom = lax.ppermute(coadd[:r, :], "skyy", up)
    vert = mm3(g_mid, split(coadd))
    vert = vert + (mm3(g_head, split(top)) + mm3(g_tail, split(bottom)))
    west = lax.ppermute(vert[:, -r:].T, "skyx", right)
    east = lax.ppermute(vert[:, :r].T, "skyx", left)
    on_cols = (((1,), (1,)), ((), ()))
    by_rows = (((0,), (1,)), ((), ()))
    result = mm3(split(vert), g_mid, on_cols)
    return result + (mm3(split(west), g_head, by_rows) + mm3(split(east), g_tail, by_rows))


def body(tiles, coeffs, weights, tile_slot, slot_offset):
    count = tiles.shape[1]
    size = tiles.shape[2]
    columns = lax.axis_size("skyx")
    slots = columns * CAP
    patch = PATCH
    basis = jnp.asarray(band_matrices(size))
    own_tiles = tiles[0]
    own_coeffs = coeffs[0]
    own_weight = weights[0]
    own_slot = tile_slot[0]
    offsets = slot_offset[:, 0, :]
    hits = own_slot[None, :] == jnp.arange(slots, dtype=jnp.int32)[:, None]
    present = jnp.any(hits, axis=1)
    which = jnp.sum(jnp.where(hits, jnp.arange(count, dtype=jnp.int32)[None, :], 0), axis=1)
    which = jnp.where(present, which, count)
    own_matched = match_all(own_tiles, own_coeffs, basis)
    extra = 16
    line = jnp.arange(extra, dtype=jnp.int32)[None, :, None] == 0
    weight_rows = jnp.where(
        line, own_weight[:, None, None], jnp.zeros((), jnp.bfloat16)
    ) * jnp.ones((1, 1, size), jnp.bfloat16)
    carry = jnp.concatenate([own_matched, weight_rows], axis=1)
    carry = jnp.concatenate([carry, jnp.zeros((1, size + extra, size), jnp.bfloat16)], axis=0)
    send = carry[which].reshape(columns, CAP, size + extra, size)
    recv = lax.all_to_all(send, "skyx", split_axis=0, concat_axis=0, tiled=True)
    recv = recv.reshape(slots, size + extra, size)
    matched = recv[:, :size, :]
    recv_weight = recv[:, size, 0]
    coadd = coadd_patch(matched, recv_weight, offsets, patch)
    detection = detect(coadd)
    return (coadd, detection)


def solution(mesh):
    in_specs = (
        P("skyy", "skyx", None, None),
        P("skyy", "skyx", None, None, None),
        P("skyy", "skyx"),
        P("skyy", "skyx"),
        P(None, "skyy", "skyx"),
    )
    out_specs = (P("skyy", "skyx"), P("skyy", "skyx"))
    return jax.shard_map(body, mesh=mesh, in_specs=in_specs, out_specs=out_specs, check_vma=False)
```

```python
import numpy as np
import jax
import jax.numpy as jnp
from jax import lax
from jax.sharding import PartitionSpec as P

NB = 5
REACH = 10
CAP = 2
PATCH = 512


basis_widths = (1.0, 1.8, 2.6, 3.6, 5.0)
detect_width = 2.5


def band_matrices(size):
    rows = np.arange(size, dtype=np.int32)[:, None]
    cols = np.arange(size, dtype=np.int32)[None, :]
    gap = (cols - rows).astype(np.float32)
    inside = np.abs(cols - rows) <= REACH
    taps = np.arange(-REACH, REACH + 1).astype(np.float32)
    mats = []
    for width in basis_widths:
        scale = np.float32(2.0 * width * width)
        total = np.sum(np.exp(-taps * taps / scale), dtype=np.float32)
        mats.append(np.where(inside, np.exp(-gap * gap / scale) / total, np.float32(0.0)))
    return np.stack(mats).astype(np.float32).astype(jnp.bfloat16)


def detect_band(out_size, in_size):
    taps = jnp.arange(-REACH, REACH + 1).astype(jnp.float32)
    scale = 2.0 * detect_width * detect_width
    total = jnp.sum(jnp.exp(-taps * taps / scale))
    rows = jnp.arange(out_size, dtype=jnp.int32)[:, None]
    cols = jnp.arange(in_size, dtype=jnp.int32)[None, :]
    gap = cols - rows
    inside = (gap >= 0) & (gap <= 2 * REACH)
    tap = (gap - REACH).astype(jnp.float32)
    return jnp.where(inside, jnp.exp(-tap * tap / scale) / total, 0.0)


def match_all(tiles, coeffs, basis):
    vert = jnp.einsum(
        "bij,mjk->mbik", basis, tiles, preferred_element_type=jnp.float32
    ).astype(jnp.bfloat16)
    horiz = jnp.einsum("mbik,bjk->mbij", vert, basis, preferred_element_type=jnp.float32)
    return jnp.sum(coeffs.astype(jnp.float32) * horiz, axis=1).astype(jnp.bfloat16)


def coadd_parts(matched, slot_weight, offsets, patch):
    slot_count = matched.shape[0]
    size = matched.shape[1]
    local = jnp.arange(size, dtype=jnp.int32)
    pixel = jnp.arange(patch, dtype=jnp.int32)
    col_hit = offsets[1][:, None, None] + local[None, :, None] == pixel[None, None, :]
    row_hit = offsets[0][None, :, None] + local[None, None, :] == pixel[:, None, None]
    col_place = col_hit.astype(jnp.bfloat16)
    shifted = jnp.einsum(
        "sij,sjq->siq", matched, col_place, preferred_element_type=jnp.float32
    ).astype(jnp.bfloat16)
    zero_weight = jnp.zeros((), jnp.bfloat16)
    row_place = jnp.where(row_hit, slot_weight[None, :, None], zero_weight)
    row_cover = jnp.where(jnp.any(row_hit, axis=2), slot_weight[None, :], zero_weight)
    col_cover = jnp.any(col_hit, axis=1).astype(jnp.bfloat16)
    return (
        row_place.reshape(patch, slot_count * size),
        shifted.reshape(slot_count * size, patch),
        row_cover,
        col_cover,
    )


def coadd_block(parts, rows=None, cols=None):
    row_place, shifted, row_cover, col_cover = parts
    if rows is not None:
        row_place = row_place[rows]
        row_cover = row_cover[rows]
    if cols is not None:
        shifted = shifted[:, cols]
        col_cover = col_cover[:, cols]
    numer = jnp.dot(row_place, shifted, preferred_element_type=jnp.float32)
    cover = jnp.dot(row_cover, col_cover, preferred_element_type=jnp.float32)
    return numer / (1.0 + cover)


def split(x):
    hi = lax.reduce_precision(x, exponent_bits=8, mantissa_bits=7)
    return hi.astype(jnp.bfloat16), (x - hi).astype(jnp.bfloat16)


def mm3(a, b, dims=(((1,), (0,)), ((), ()))):
    ah, al = a
    bh, bl = b

    def one(x, y):
        return lax.dot_general(x, y, dims, preferred_element_type=jnp.float32)

    return one(ah, bh) + (one(al, bh) + one(ah, bl))


def detect(parts, patch):
    ny = lax.axis_size("skyy")
    nx = lax.axis_size("skyx")
    r = REACH
    band = detect_band(patch, patch + 2 * r)
    g_head = split(band[:, :r])
    g_mid = split(band[:, r:patch + r])
    g_tail = split(band[:, patch + r:])
    down = [(i, i + 1) for i in range(ny - 1)]
    up = [(i + 1, i) for i in range(ny - 1)]
    right = [(j, j + 1) for j in range(nx - 1)]
    left = [(j + 1, j) for j in range(nx - 1)]
    top = lax.ppermute(coadd_block(parts, rows=slice(patch - r, patch)), "skyy", down)
    bottom = lax.ppermute(coadd_block(parts, rows=slice(0, r)), "skyy", up)
    on_cols = (((1,), (1,)), ((), ()))
    by_rows = (((0,), (1,)), ((), ()))

    def vertical(own, above, below):
        inner = mm3(g_mid, split(own))
        return inner + (mm3(g_head, split(above)) + mm3(g_tail, split(below)))

    first = vertical(coadd_block(parts, cols=slice(0, r)), top[:, :r], bottom[:, :r])
    last = vertical(
        coadd_block(parts, cols=slice(patch - r, patch)), top[:, patch - r:], bottom[:, patch - r:]
    )
    west = lax.ppermute(last.T, "skyx", right)
    east = lax.ppermute(first.T, "skyx", left)
    coadd = coadd_block(parts)
    vert = vertical(coadd, top, bottom)
    result = mm3(split(vert), g_mid, on_cols)
    result = result + (mm3(split(west), g_head, by_rows) + mm3(split(east), g_tail, by_rows))
    return coadd, result


def body(tiles, coeffs, weights, tile_slot, slot_offset):
    count = tiles.shape[1]
    size = tiles.shape[2]
    columns = lax.axis_size("skyx")
    slots = columns * CAP
    patch = PATCH
    basis = jnp.asarray(band_matrices(size))
    own_tiles = tiles[0]
    own_coeffs = coeffs[0]
    own_weight = weights[0]
    own_slot = tile_slot[0]
    offsets = slot_offset[:, 0, :]
    hits = own_slot[None, :] == jnp.arange(slots, dtype=jnp.int32)[:, None]
    present = jnp.any(hits, axis=1)
    which = jnp.sum(jnp.where(hits, jnp.arange(count, dtype=jnp.int32)[None, :], 0), axis=1)
    which = jnp.where(present, which, count)
    own_matched = match_all(own_tiles, own_coeffs, basis)
    extra = 16
    line = jnp.arange(extra, dtype=jnp.int32)[None, :, None] == 0
    weight_rows = jnp.where(
        line, own_weight[:, None, None], jnp.zeros((), jnp.bfloat16)
    ) * jnp.ones((1, 1, size), jnp.bfloat16)
    carry = jnp.concatenate([own_matched, weight_rows], axis=1)
    carry = jnp.concatenate([carry, jnp.zeros((1, size + extra, size), jnp.bfloat16)], axis=0)
    send = carry[which].reshape(columns, CAP, size + extra, size)
    recv = lax.all_to_all(send, "skyx", split_axis=0, concat_axis=0, tiled=True)
    recv = recv.reshape(slots, size + extra, size)
    matched = recv[:, :size, :]
    recv_weight = recv[:, size, 0]
    parts = coadd_parts(matched, recv_weight, offsets, patch)
    coadd, detection = detect(parts, patch)
    return (coadd, detection)


def solution(mesh):
    in_specs = (
        P("skyy", "skyx", None, None),
        P("skyy", "skyx", None, None, None),
        P("skyy", "skyx"),
        P("skyy", "skyx"),
        P(None, "skyy", "skyx"),
    )
    out_specs = (P("skyy", "skyx"), P("skyy", "skyx"))
    return jax.shard_map(body, mesh=mesh, in_specs=in_specs, out_specs=out_specs, check_vma=False)
```

```python
import numpy as np
import jax
import jax.numpy as jnp
from jax import lax
from jax.experimental import pallas as pl
from jax.experimental.pallas import tpu as pltpu
from jax.sharding import PartitionSpec as P

NB = 5
REACH = 10
CAP = 2
PATCH = 512


basis_widths = (1.0, 1.8, 2.6, 3.6, 5.0)
detect_width = 2.5


def band_matrices(size):
    rows = np.arange(size, dtype=np.int32)[:, None]
    cols = np.arange(size, dtype=np.int32)[None, :]
    gap = (cols - rows).astype(np.float32)
    inside = np.abs(cols - rows) <= REACH
    taps = np.arange(-REACH, REACH + 1).astype(np.float32)
    mats = []
    for width in basis_widths:
        scale = np.float32(2.0 * width * width)
        total = np.sum(np.exp(-taps * taps / scale), dtype=np.float32)
        mats.append(np.where(inside, np.exp(-gap * gap / scale) / total, np.float32(0.0)))
    return np.stack(mats).astype(np.float32).astype(jnp.bfloat16)


def detect_band(out_size, in_size):
    taps = jnp.arange(-REACH, REACH + 1).astype(jnp.float32)
    scale = 2.0 * detect_width * detect_width
    total = jnp.sum(jnp.exp(-taps * taps / scale))
    rows = jnp.arange(out_size, dtype=jnp.int32)[:, None]
    cols = jnp.arange(in_size, dtype=jnp.int32)[None, :]
    gap = cols - rows
    inside = (gap >= 0) & (gap <= 2 * REACH)
    tap = (gap - REACH).astype(jnp.float32)
    return jnp.where(inside, jnp.exp(-tap * tap / scale) / total, 0.0)


def match_kernel(slot_ref, weight_ref, tile_ref, coeff_ref, basis_ref, zero_ref, out_ref):
    j = pl.program_id(0)
    size = tile_ref.shape[-1]
    tile = tile_ref[0, 0]
    total = jnp.zeros((size, size), jnp.float32)
    for b in range(NB):
        band = basis_ref[b]
        vert = jnp.dot(band, tile, preferred_element_type=jnp.float32).astype(jnp.bfloat16)
        horiz = lax.dot_general(
            vert, band, (((1,), (1,)), ((), ())), preferred_element_type=jnp.float32
        )
        total = total + coeff_ref[0, 0, b].astype(jnp.float32) * horiz
    out_ref[0, :size, :] = total.astype(jnp.bfloat16)
    extra = out_ref.shape[1] - size
    line = lax.broadcasted_iota(jnp.int32, (extra, size), 0)
    out_ref[0, size:, :] = jnp.where(line == 0, weight_ref[j], 0.0).astype(jnp.bfloat16)


def match_into_slots(tiles, coeffs, weights, own_slot, basis, slots, extra):
    count = tiles.shape[1]
    size = tiles.shape[2]
    zeros = jnp.zeros((slots, size + extra, size), jnp.bfloat16)
    grid_spec = pltpu.PrefetchScalarGridSpec(
        num_scalar_prefetch=2,
        grid=(count,),
        in_specs=[
            pl.BlockSpec((1, 1, size, size), lambda j, slot, w: (0, j, 0, 0)),
            pl.BlockSpec((1, 1, NB, size, size), lambda j, slot, w: (0, j, 0, 0, 0)),
            pl.BlockSpec((NB, size, size), lambda j, slot, w: (0, 0, 0)),
            pl.BlockSpec(memory_space=pl.ANY),
        ],
        out_specs=pl.BlockSpec((1, size + extra, size), lambda j, slot, w: (slot[j], 0, 0)),
    )
    flops = count * NB * 4 * size * size * size
    moved = count * (NB + 1) * size * size * 2 + count * (size + extra) * size * 2
    return pl.pallas_call(
        match_kernel,
        out_shape=jax.ShapeDtypeStruct((slots, size + extra, size), jnp.bfloat16),
        grid_spec=grid_spec,
        input_output_aliases={5: 0},
        cost_estimate=pl.CostEstimate(flops=flops, bytes_accessed=moved, transcendentals=0),
    )(own_slot, weights, tiles, coeffs, basis, zeros)


def coadd_patch(matched, slot_weight, offsets, patch):
    slot_count = matched.shape[0]
    size = matched.shape[1]
    local = jnp.arange(size, dtype=jnp.int32)
    pixel = jnp.arange(patch, dtype=jnp.int32)
    col_hit = offsets[1][:, None, None] + local[None, :, None] == pixel[None, None, :]
    row_hit = offsets[0][None, :, None] + local[None, None, :] == pixel[:, None, None]
    col_place = col_hit.astype(jnp.bfloat16)
    shifted = jnp.einsum(
        "sij,sjq->siq", matched, col_place, preferred_element_type=jnp.float32
    ).astype(jnp.bfloat16)
    zero_weight = jnp.zeros((), jnp.bfloat16)
    row_place = jnp.where(row_hit, slot_weight[None, :, None], zero_weight)
    numer = jnp.dot(
        row_place.reshape(patch, slot_count * size),
        shifted.reshape(slot_count * size, patch),
        preferred_element_type=jnp.float32,
    )
    row_cover = jnp.where(jnp.any(row_hit, axis=2), slot_weight[None, :], zero_weight)
    col_cover = jnp.any(col_hit, axis=1).astype(jnp.bfloat16)
    cover = jnp.dot(row_cover, col_cover, preferred_element_type=jnp.float32)
    return numer / (1.0 + cover)


def split(x):
    hi = lax.reduce_precision(x, exponent_bits=8, mantissa_bits=7)
    return hi.astype(jnp.bfloat16), (x - hi).astype(jnp.bfloat16)


def mm3(a, b, dims=(((1,), (0,)), ((), ()))):
    ah, al = a
    bh, bl = b

    def one(x, y):
        return lax.dot_general(x, y, dims, preferred_element_type=jnp.float32)

    return one(ah, bh) + (one(al, bh) + one(ah, bl))


def detect(coadd):
    ny = lax.axis_size("skyy")
    nx = lax.axis_size("skyx")
    r = REACH
    patch = coadd.shape[0]
    band = detect_band(patch, patch + 2 * r)
    g_head = split(band[:, :r])
    g_mid = split(band[:, r:patch + r])
    g_tail = split(band[:, patch + r:])
    down = [(i, i + 1) for i in range(ny - 1)]
    up = [(i + 1, i) for i in range(ny - 1)]
    right = [(j, j + 1) for j in range(nx - 1)]
    left = [(j + 1, j) for j in range(nx - 1)]
    top = lax.ppermute(coadd[-r:, :], "skyy", down)
    bottom = lax.ppermute(coadd[:r, :], "skyy", up)
    vert = mm3(g_mid, split(coadd))
    vert = vert + (mm3(g_head, split(top)) + mm3(g_tail, split(bottom)))
    west = lax.ppermute(vert[:, -r:].T, "skyx", right)
    east = lax.ppermute(vert[:, :r].T, "skyx", left)
    on_cols = (((1,), (1,)), ((), ()))
    by_rows = (((0,), (1,)), ((), ()))
    result = mm3(split(vert), g_mid, on_cols)
    return result + (mm3(split(west), g_head, by_rows) + mm3(split(east), g_tail, by_rows))


def body(tiles, coeffs, weights, tile_slot, slot_offset):
    count = tiles.shape[1]
    size = tiles.shape[2]
    columns = lax.axis_size("skyx")
    slots = columns * CAP
    patch = PATCH
    basis = jnp.asarray(band_matrices(size))
    own_tiles = tiles[0]
    own_coeffs = coeffs[0]
    own_weight = weights[0]
    own_slot = tile_slot[0]
    offsets = slot_offset[:, 0, :]
    extra = 16
    send = match_into_slots(
        tiles, coeffs, own_weight.astype(jnp.float32), own_slot, basis, slots, extra
    ).reshape(columns, CAP, size + extra, size)
    recv = lax.all_to_all(send, "skyx", split_axis=0, concat_axis=0, tiled=True)
    recv = recv.reshape(slots, size + extra, size)
    matched = recv[:, :size, :]
    recv_weight = recv[:, size, 0]
    coadd = coadd_patch(matched, recv_weight, offsets, patch)
    detection = detect(coadd)
    return (coadd, detection)


def solution(mesh):
    in_specs = (
        P("skyy", "skyx", None, None),
        P("skyy", "skyx", None, None, None),
        P("skyy", "skyx"),
        P("skyy", "skyx"),
        P(None, "skyy", "skyx"),
    )
    out_specs = (P("skyy", "skyx"), P("skyy", "skyx"))
    return jax.shard_map(body, mesh=mesh, in_specs=in_specs, out_specs=out_specs, check_vma=False)
```

```python
import numpy as np
import jax
import jax.numpy as jnp
from jax import lax
from jax.sharding import PartitionSpec as P

NB = 5
REACH = 10
CAP = 2
PATCH = 512


basis_widths = (1.0, 1.8, 2.6, 3.6, 5.0)
detect_width = 2.5


def band_matrices(size):
    rows = np.arange(size, dtype=np.int32)[:, None]
    cols = np.arange(size, dtype=np.int32)[None, :]
    gap = (cols - rows).astype(np.float32)
    inside = np.abs(cols - rows) <= REACH
    taps = np.arange(-REACH, REACH + 1).astype(np.float32)
    mats = []
    for width in basis_widths:
        scale = np.float32(2.0 * width * width)
        total = np.sum(np.exp(-taps * taps / scale), dtype=np.float32)
        mats.append(np.where(inside, np.exp(-gap * gap / scale) / total, np.float32(0.0)))
    return np.stack(mats).astype(np.float32).astype(jnp.bfloat16)


def detect_band(out_size, in_size):
    taps = jnp.arange(-REACH, REACH + 1).astype(jnp.float32)
    scale = 2.0 * detect_width * detect_width
    total = jnp.sum(jnp.exp(-taps * taps / scale))
    rows = jnp.arange(out_size, dtype=jnp.int32)[:, None]
    cols = jnp.arange(in_size, dtype=jnp.int32)[None, :]
    gap = cols - rows
    inside = (gap >= 0) & (gap <= 2 * REACH)
    tap = (gap - REACH).astype(jnp.float32)
    return jnp.where(inside, jnp.exp(-tap * tap / scale) / total, 0.0)


def match_all(tiles, coeffs, basis):
    vert = jnp.einsum(
        "bij,mjk->mbik", basis, tiles, preferred_element_type=jnp.float32
    ).astype(jnp.bfloat16)
    horiz = jnp.einsum("mbik,bjk->mbij", vert, basis, preferred_element_type=jnp.float32)
    return jnp.sum(coeffs.astype(jnp.float32) * horiz, axis=1).astype(jnp.bfloat16)


def coadd_patch(matched, slot_weight, offsets, patch):
    slot_count = matched.shape[0]
    size = matched.shape[1]
    local = jnp.arange(size, dtype=jnp.int32)
    pixel = jnp.arange(patch, dtype=jnp.int32)
    col_hit = offsets[1][:, None, None] + local[None, :, None] == pixel[None, None, :]
    row_hit = offsets[0][None, :, None] + local[None, None, :] == pixel[:, None, None]
    col_place = col_hit.astype(jnp.bfloat16)
    shifted = jnp.einsum(
        "sij,sjq->siq", matched, col_place, preferred_element_type=jnp.float32
    ).astype(jnp.bfloat16)
    zero_weight = jnp.zeros((), jnp.bfloat16)
    row_place = jnp.where(row_hit, slot_weight[None, :, None], zero_weight)
    numer = jnp.dot(
        row_place.reshape(patch, slot_count * size),
        shifted.reshape(slot_count * size, patch),
        preferred_element_type=jnp.float32,
    )
    row_cover = jnp.where(jnp.any(row_hit, axis=2), slot_weight[None, :], zero_weight)
    col_cover = jnp.any(col_hit, axis=1).astype(jnp.bfloat16)
    cover = jnp.dot(row_cover, col_cover, preferred_element_type=jnp.float32)
    return numer / (1.0 + cover)


def split(x):
    hi = lax.reduce_precision(x, exponent_bits=8, mantissa_bits=7)
    return hi.astype(jnp.bfloat16), (x - hi).astype(jnp.bfloat16)


def mm3(a, b, dims=(((1,), (0,)), ((), ()))):
    ah, al = a
    bh, bl = b

    def one(x, y):
        return lax.dot_general(x, y, dims, preferred_element_type=jnp.float32)

    return one(ah, bh) + (one(al, bh) + one(ah, bl))


def detect(coadd):
    ny = lax.axis_size("skyy")
    nx = lax.axis_size("skyx")
    r = REACH
    patch = coadd.shape[0]
    band = split(detect_band(patch, patch + 2 * r))
    down = [(i, i + 1) for i in range(ny - 1)]
    up = [(i + 1, i) for i in range(ny - 1)]
    right = [(j, j + 1) for j in range(nx - 1)]
    left = [(j + 1, j) for j in range(nx - 1)]
    top = lax.ppermute(coadd[-r:, :], "skyy", down)
    bottom = lax.ppermute(coadd[:r, :], "skyy", up)
    rows = jnp.concatenate([top, coadd, bottom], axis=0)
    vert = mm3(band, split(rows))
    west = lax.ppermute(vert[:, -r:].T, "skyx", right)
    east = lax.ppermute(vert[:, :r].T, "skyx", left)
    cols = jnp.concatenate([west.T, vert, east.T], axis=1)
    return mm3(split(cols), band, (((1,), (1,)), ((), ())))


def body(tiles, coeffs, weights, tile_slot, slot_offset):
    count = tiles.shape[1]
    size = tiles.shape[2]
    columns = lax.axis_size("skyx")
    slots = columns * CAP
    patch = PATCH
    basis = jnp.asarray(band_matrices(size))
    own_tiles = tiles[0]
    own_coeffs = coeffs[0]
    own_weight = weights[0]
    own_slot = tile_slot[0]
    offsets = slot_offset[:, 0, :]
    hits = own_slot[None, :] == jnp.arange(slots, dtype=jnp.int32)[:, None]
    present = jnp.any(hits, axis=1)
    which = jnp.sum(jnp.where(hits, jnp.arange(count, dtype=jnp.int32)[None, :], 0), axis=1)
    which = jnp.where(present, which, count)
    own_matched = match_all(own_tiles, own_coeffs, basis)
    extra = 16
    line = jnp.arange(extra, dtype=jnp.int32)[None, :, None] == 0
    weight_rows = jnp.where(
        line, own_weight[:, None, None], jnp.zeros((), jnp.bfloat16)
    ) * jnp.ones((1, 1, size), jnp.bfloat16)
    carry = jnp.concatenate([own_matched, weight_rows], axis=1)
    carry = jnp.concatenate([carry, jnp.zeros((1, size + extra, size), jnp.bfloat16)], axis=0)
    send = carry[which].reshape(columns, CAP, size + extra, size)
    recv = lax.all_to_all(send, "skyx", split_axis=0, concat_axis=0, tiled=True)
    recv = recv.reshape(slots, size + extra, size)
    matched = recv[:, :size, :]
    recv_weight = recv[:, size, 0]
    coadd = coadd_patch(matched, recv_weight, offsets, patch)
    detection = detect(coadd)
    return (coadd, detection)


def solution(mesh):
    in_specs = (
        P("skyy", "skyx", None, None),
        P("skyy", "skyx", None, None, None),
        P("skyy", "skyx"),
        P("skyy", "skyx"),
        P(None, "skyy", "skyx"),
    )
    out_specs = (P("skyy", "skyx"), P("skyy", "skyx"))
    return jax.shard_map(body, mesh=mesh, in_specs=in_specs, out_specs=out_specs, check_vma=False)
```

```python
import numpy as np
import jax
import jax.numpy as jnp
from jax import lax
from jax.sharding import PartitionSpec as P

NB = 5
REACH = 10
CAP = 2
PATCH = 512


basis_widths = (1.0, 1.8, 2.6, 3.6, 5.0)
detect_width = 2.5


def band_matrices(size):
    rows = np.arange(size, dtype=np.int32)[:, None]
    cols = np.arange(size, dtype=np.int32)[None, :]
    gap = (cols - rows).astype(np.float32)
    inside = np.abs(cols - rows) <= REACH
    taps = np.arange(-REACH, REACH + 1).astype(np.float32)
    mats = []
    for width in basis_widths:
        scale = np.float32(2.0 * width * width)
        total = np.sum(np.exp(-taps * taps / scale), dtype=np.float32)
        mats.append(np.where(inside, np.exp(-gap * gap / scale) / total, np.float32(0.0)))
    return np.stack(mats).astype(np.float32).astype(jnp.bfloat16)


def detect_band(out_size, in_size):
    taps = jnp.arange(-REACH, REACH + 1).astype(jnp.float32)
    scale = 2.0 * detect_width * detect_width
    total = jnp.sum(jnp.exp(-taps * taps / scale))
    rows = jnp.arange(out_size, dtype=jnp.int32)[:, None]
    cols = jnp.arange(in_size, dtype=jnp.int32)[None, :]
    gap = cols - rows
    inside = (gap >= 0) & (gap <= 2 * REACH)
    tap = (gap - REACH).astype(jnp.float32)
    return jnp.where(inside, jnp.exp(-tap * tap / scale) / total, 0.0)


def match_all(tiles, coeffs, basis):
    vert = jnp.einsum(
        "bij,mjk->mbik", basis, tiles, preferred_element_type=jnp.float32
    ).astype(jnp.bfloat16)
    horiz = jnp.einsum("mbik,bjk->mbij", vert, basis, preferred_element_type=jnp.float32)
    return jnp.sum(coeffs.astype(jnp.float32) * horiz, axis=1).astype(jnp.bfloat16)


def coadd_patch(matched, slot_weight, offsets, patch):
    slot_count = matched.shape[0]
    size = matched.shape[1]
    local = jnp.arange(size, dtype=jnp.int32)
    pixel = jnp.arange(patch, dtype=jnp.int32)
    col_hit = offsets[1][:, None, None] + local[None, :, None] == pixel[None, None, :]
    row_hit = offsets[0][None, :, None] + local[None, None, :] == pixel[:, None, None]
    col_place = col_hit.astype(jnp.bfloat16)
    shifted = jnp.einsum(
        "sij,sjq->siq", matched, col_place, preferred_element_type=jnp.float32
    ).astype(jnp.bfloat16)
    zero_weight = jnp.zeros((), jnp.bfloat16)
    row_place = jnp.where(row_hit, slot_weight[None, :, None], zero_weight)
    numer = jnp.dot(
        row_place.reshape(patch, slot_count * size),
        shifted.reshape(slot_count * size, patch),
        preferred_element_type=jnp.float32,
    )
    row_cover = jnp.where(jnp.any(row_hit, axis=2), slot_weight[None, :], zero_weight)
    col_cover = jnp.any(col_hit, axis=1).astype(jnp.bfloat16)
    cover = jnp.dot(row_cover, col_cover, preferred_element_type=jnp.float32)
    return numer / (1.0 + cover)


def split(x):
    hi = lax.reduce_precision(x, exponent_bits=8, mantissa_bits=7)
    return hi.astype(jnp.bfloat16), (x - hi).astype(jnp.bfloat16)


def mm3(a, b, dims=(((1,), (0,)), ((), ()))):
    ah, al = a
    bh, bl = b

    def one(x, y):
        return lax.dot_general(x, y, dims, preferred_element_type=jnp.float32)

    return one(ah, bh) + (one(al, bh) + one(ah, bl))


def detect(coadd):
    ny = lax.axis_size("skyy")
    nx = lax.axis_size("skyx")
    r = REACH
    patch = coadd.shape[0]
    hi, lo = split(detect_band(patch, patch + 2 * r))
    mid = jnp.concatenate([hi[:, r:patch + r], lo[:, r:patch + r]], axis=1)
    edge = jnp.concatenate(
        [hi[:, :r], hi[:, patch + r:], lo[:, :r], lo[:, patch + r:]], axis=1
    )
    down = [(i, i + 1) for i in range(ny - 1)]
    up = [(i + 1, i) for i in range(ny - 1)]
    right = [(j, j + 1) for j in range(nx - 1)]
    left = [(j + 1, j) for j in range(nx - 1)]
    f32 = jnp.float32
    own = coadd.astype(jnp.bfloat16)
    top = lax.ppermute(own[-r:, :], "skyy", down)
    bottom = lax.ppermute(own[:r, :], "skyy", up)
    vert = jnp.dot(mid, jnp.concatenate([own, own], axis=0), preferred_element_type=f32)
    rim = jnp.concatenate([top, bottom, top, bottom], axis=0)
    vert = vert + jnp.dot(edge, rim, preferred_element_type=f32)
    vown = vert.astype(jnp.bfloat16)
    west = lax.ppermute(vown[:, -r:].T, "skyx", right)
    east = lax.ppermute(vown[:, :r].T, "skyx", left)
    on_cols = (((1,), (1,)), ((), ()))
    by_rows = (((0,), (1,)), ((), ()))
    result = lax.dot_general(
        jnp.concatenate([vown, vown], axis=1), mid, on_cols, preferred_element_type=f32
    )
    side = jnp.concatenate([west, east, west, east], axis=0)
    return result + lax.dot_general(side, edge, by_rows, preferred_element_type=f32)


def body(tiles, coeffs, weights, tile_slot, slot_offset):
    count = tiles.shape[1]
    size = tiles.shape[2]
    columns = lax.axis_size("skyx")
    slots = columns * CAP
    patch = PATCH
    basis = jnp.asarray(band_matrices(size))
    own_tiles = tiles[0]
    own_coeffs = coeffs[0]
    own_weight = weights[0]
    own_slot = tile_slot[0]
    offsets = slot_offset[:, 0, :]
    hits = own_slot[None, :] == jnp.arange(slots, dtype=jnp.int32)[:, None]
    present = jnp.any(hits, axis=1)
    which = jnp.sum(jnp.where(hits, jnp.arange(count, dtype=jnp.int32)[None, :], 0), axis=1)
    which = jnp.where(present, which, count)
    own_matched = match_all(own_tiles, own_coeffs, basis)
    extra = 16
    line = jnp.arange(extra, dtype=jnp.int32)[None, :, None] == 0
    weight_rows = jnp.where(
        line, own_weight[:, None, None], jnp.zeros((), jnp.bfloat16)
    ) * jnp.ones((1, 1, size), jnp.bfloat16)
    carry = jnp.concatenate([own_matched, weight_rows], axis=1)
    carry = jnp.concatenate([carry, jnp.zeros((1, size + extra, size), jnp.bfloat16)], axis=0)
    send = carry[which].reshape(columns, CAP, size + extra, size)
    recv = lax.all_to_all(send, "skyx", split_axis=0, concat_axis=0, tiled=True)
    recv = recv.reshape(slots, size + extra, size)
    matched = recv[:, :size, :]
    recv_weight = recv[:, size, 0]
    coadd = coadd_patch(matched, recv_weight, offsets, patch)
    detection = detect(coadd)
    return (coadd, detection)


def solution(mesh):
    in_specs = (
        P("skyy", "skyx", None, None),
        P("skyy", "skyx", None, None, None),
        P("skyy", "skyx"),
        P("skyy", "skyx"),
        P(None, "skyy", "skyx"),
    )
    out_specs = (P("skyy", "skyx"), P("skyy", "skyx"))
    return jax.shard_map(body, mesh=mesh, in_specs=in_specs, out_specs=out_specs, check_vma=False)
```

```python
import numpy as np
import jax
import jax.numpy as jnp
from jax import lax
from jax.sharding import PartitionSpec as P

NB = 5
REACH = 10
CAP = 2
PATCH = 512


basis_widths = (1.0, 1.8, 2.6, 3.6, 5.0)
detect_width = 2.5


def band_matrices(size):
    rows = np.arange(size, dtype=np.int32)[:, None]
    cols = np.arange(size, dtype=np.int32)[None, :]
    gap = (cols - rows).astype(np.float32)
    inside = np.abs(cols - rows) <= REACH
    taps = np.arange(-REACH, REACH + 1).astype(np.float32)
    mats = []
    for width in basis_widths:
        scale = np.float32(2.0 * width * width)
        total = np.sum(np.exp(-taps * taps / scale), dtype=np.float32)
        mats.append(np.where(inside, np.exp(-gap * gap / scale) / total, np.float32(0.0)))
    return np.stack(mats).astype(np.float32).astype(jnp.bfloat16)


def detect_band(out_size, in_size):
    taps = jnp.arange(-REACH, REACH + 1).astype(jnp.float32)
    scale = 2.0 * detect_width * detect_width
    total = jnp.sum(jnp.exp(-taps * taps / scale))
    rows = jnp.arange(out_size, dtype=jnp.int32)[:, None]
    cols = jnp.arange(in_size, dtype=jnp.int32)[None, :]
    gap = cols - rows
    inside = (gap >= 0) & (gap <= 2 * REACH)
    tap = (gap - REACH).astype(jnp.float32)
    return jnp.where(inside, jnp.exp(-tap * tap / scale) / total, 0.0)


def match_all(tiles, coeffs, basis):
    vert = jnp.einsum(
        "bij,mjk->mbik", basis, tiles, preferred_element_type=jnp.float32
    ).astype(jnp.bfloat16)
    horiz = jnp.einsum("mbik,bjk->mbij", vert, basis, preferred_element_type=jnp.float32)
    return jnp.sum(coeffs.astype(jnp.float32) * horiz, axis=1).astype(jnp.bfloat16)


def coadd_patch(matched, slot_weight, offsets, patch):
    slot_count = matched.shape[0]
    size = matched.shape[1]
    local = jnp.arange(size, dtype=jnp.int32)
    pixel = jnp.arange(patch, dtype=jnp.int32)
    col_hit = offsets[1][:, None, None] + local[None, :, None] == pixel[None, None, :]
    row_hit = offsets[0][None, :, None] + local[None, None, :] == pixel[:, None, None]
    col_place = col_hit.astype(jnp.bfloat16)
    shifted = jnp.einsum(
        "sij,sjq->siq", matched, col_place, preferred_element_type=jnp.float32
    ).astype(jnp.bfloat16)
    zero_weight = jnp.zeros((), jnp.bfloat16)
    row_place = jnp.where(row_hit, slot_weight[None, :, None], zero_weight)
    numer = jnp.dot(
        row_place.reshape(patch, slot_count * size),
        shifted.reshape(slot_count * size, patch),
        preferred_element_type=jnp.float32,
    )
    row_gap = pixel[:, None] - offsets[0][None, :]
    col_gap = pixel[None, :] - offsets[1][:, None]
    row_in = (row_gap >= 0) & (row_gap < size)
    col_in = (col_gap >= 0) & (col_gap < size)
    row_cover = jnp.where(row_in, slot_weight[None, :], zero_weight)
    col_cover = col_in.astype(jnp.bfloat16)
    cover = jnp.dot(row_cover, col_cover, preferred_element_type=jnp.float32)
    return numer / (1.0 + cover)


def split(x):
    hi = lax.reduce_precision(x, exponent_bits=8, mantissa_bits=7)
    return hi.astype(jnp.bfloat16), (x - hi).astype(jnp.bfloat16)


def mm3(a, b, dims=(((1,), (0,)), ((), ()))):
    ah, al = a
    bh, bl = b

    def one(x, y):
        return lax.dot_general(x, y, dims, preferred_element_type=jnp.float32)

    return one(ah, bh) + (one(al, bh) + one(ah, bl))


def detect_filters(patch):
    r = REACH
    hi, lo = split(detect_band(patch, patch + 2 * r))
    mid = jnp.concatenate([hi[:, r:patch + r], lo[:, r:patch + r]], axis=1)
    edge = jnp.concatenate(
        [hi[:, :r], hi[:, patch + r:], lo[:, :r], lo[:, patch + r:]], axis=1
    )
    return mid, edge


def detect(coadd, mid, edge):
    ny = lax.axis_size("skyy")
    nx = lax.axis_size("skyx")
    r = REACH
    patch = coadd.shape[0]
    down = [(i, i + 1) for i in range(ny - 1)]
    up = [(i + 1, i) for i in range(ny - 1)]
    right = [(j, j + 1) for j in range(nx - 1)]
    left = [(j + 1, j) for j in range(nx - 1)]
    f32 = jnp.float32
    own = coadd.astype(jnp.bfloat16)
    top = lax.ppermute(own[-r:, :], "skyy", down)
    bottom = lax.ppermute(own[:r, :], "skyy", up)
    vert = jnp.dot(mid, jnp.concatenate([own, own], axis=0), preferred_element_type=f32)
    rim = jnp.concatenate([top, bottom, top, bottom], axis=0)
    vert = vert + jnp.dot(edge, rim, preferred_element_type=f32)
    vown = vert.astype(jnp.bfloat16)
    west = lax.ppermute(vown[:, -r:].T, "skyx", right)
    east = lax.ppermute(vown[:, :r].T, "skyx", left)
    on_cols = (((1,), (1,)), ((), ()))
    by_rows = (((0,), (1,)), ((), ()))
    result = lax.dot_general(
        jnp.concatenate([vown, vown], axis=1), mid, on_cols, preferred_element_type=f32
    )
    side = jnp.concatenate([west, east, west, east], axis=0)
    return result + lax.dot_general(side, edge, by_rows, preferred_element_type=f32)


def body(tiles, coeffs, weights, tile_slot, slot_offset):
    count = tiles.shape[1]
    size = tiles.shape[2]
    columns = lax.axis_size("skyx")
    slots = columns * CAP
    patch = PATCH
    basis = jnp.asarray(band_matrices(size))
    own_tiles = tiles[0]
    own_coeffs = coeffs[0]
    own_weight = weights[0]
    own_slot = tile_slot[0]
    offsets = slot_offset[:, 0, :]
    hits = own_slot[None, :] == jnp.arange(slots, dtype=jnp.int32)[:, None]
    present = jnp.any(hits, axis=1)
    which = jnp.sum(jnp.where(hits, jnp.arange(count, dtype=jnp.int32)[None, :], 0), axis=1)
    which = jnp.where(present, which, count)
    own_matched = match_all(own_tiles, own_coeffs, basis)
    extra = 16
    line = jnp.arange(extra, dtype=jnp.int32)[None, :, None] == 0
    weight_rows = jnp.where(
        line, own_weight[:, None, None], jnp.zeros((), jnp.bfloat16)
    ) * jnp.ones((1, 1, size), jnp.bfloat16)
    carry = jnp.concatenate([own_matched, weight_rows], axis=1)
    carry = jnp.concatenate([carry, jnp.zeros((1, size + extra, size), jnp.bfloat16)], axis=0)
    send = carry[which].reshape(columns, CAP, size + extra, size)
    filters = detect_filters(patch)
    send, filters = lax.optimization_barrier((send, filters))
    recv = lax.all_to_all(send, "skyx", split_axis=0, concat_axis=0, tiled=True)
    recv, offsets, filters = lax.optimization_barrier((recv, offsets, filters))
    recv = recv.reshape(slots, size + extra, size)
    matched = recv[:, :size, :]
    recv_weight = recv[:, size, 0]
    coadd = coadd_patch(matched, recv_weight, offsets, patch)
    detection = detect(coadd, *filters)
    return (coadd, detection)


def solution(mesh):
    in_specs = (
        P("skyy", "skyx", None, None),
        P("skyy", "skyx", None, None, None),
        P("skyy", "skyx"),
        P("skyy", "skyx"),
        P(None, "skyy", "skyx"),
    )
    out_specs = (P("skyy", "skyx"), P("skyy", "skyx"))
    return jax.shard_map(body, mesh=mesh, in_specs=in_specs, out_specs=out_specs, check_vma=False)
```

```python
import numpy as np
import jax
import jax.numpy as jnp
from jax import lax
from jax.sharding import PartitionSpec as P

NB = 5
REACH = 10
CAP = 2
PATCH = 512


basis_widths = (1.0, 1.8, 2.6, 3.6, 5.0)
detect_width = 2.5


def band_matrices(size):
    rows = np.arange(size, dtype=np.int32)[:, None]
    cols = np.arange(size, dtype=np.int32)[None, :]
    gap = (cols - rows).astype(np.float32)
    inside = np.abs(cols - rows) <= REACH
    taps = np.arange(-REACH, REACH + 1).astype(np.float32)
    mats = []
    for width in basis_widths:
        scale = np.float32(2.0 * width * width)
        total = np.sum(np.exp(-taps * taps / scale), dtype=np.float32)
        mats.append(np.where(inside, np.exp(-gap * gap / scale) / total, np.float32(0.0)))
    return np.stack(mats).astype(np.float32).astype(jnp.bfloat16)


def match_all(tiles, coeffs, basis):
    vert = jnp.einsum(
        "bij,mjk->mbik", basis, tiles, preferred_element_type=jnp.float32
    ).astype(jnp.bfloat16)
    horiz = jnp.einsum("mbik,bjk->mbij", vert, basis, preferred_element_type=jnp.float32)
    return jnp.sum(coeffs.astype(jnp.float32) * horiz, axis=1).astype(jnp.bfloat16)


def coadd_patch(matched, slot_weight, offsets, patch):
    slot_count = matched.shape[0]
    size = matched.shape[1]
    local = jnp.arange(size, dtype=jnp.int32)
    pixel = jnp.arange(patch, dtype=jnp.int32)
    col_hit = offsets[1][:, None, None] + local[None, :, None] == pixel[None, None, :]
    row_hit = offsets[0][None, :, None] + local[None, None, :] == pixel[:, None, None]
    col_place = col_hit.astype(jnp.bfloat16)
    shifted = jnp.einsum(
        "sij,sjq->siq", matched, col_place, preferred_element_type=jnp.float32
    ).astype(jnp.bfloat16)
    zero_weight = jnp.zeros((), jnp.bfloat16)
    row_place = jnp.where(row_hit, slot_weight[None, :, None], zero_weight)
    numer = jnp.dot(
        row_place.reshape(patch, slot_count * size),
        shifted.reshape(slot_count * size, patch),
        preferred_element_type=jnp.float32,
    )
    row_gap = pixel[:, None] - offsets[0][None, :]
    col_gap = pixel[None, :] - offsets[1][:, None]
    row_in = (row_gap >= 0) & (row_gap < size)
    col_in = (col_gap >= 0) & (col_gap < size)
    row_cover = jnp.where(row_in, slot_weight[None, :], zero_weight)
    col_cover = col_in.astype(jnp.bfloat16)
    cover = jnp.dot(row_cover, col_cover, preferred_element_type=jnp.float32)
    return numer / (1.0 + cover)


def split(x):
    hi = lax.reduce_precision(x, exponent_bits=8, mantissa_bits=7)
    return hi.astype(jnp.bfloat16), (x - hi).astype(jnp.bfloat16)


def mm3(a, b, dims=(((1,), (0,)), ((), ()))):
    ah, al = a
    bh, bl = b

    def one(x, y):
        return lax.dot_general(x, y, dims, preferred_element_type=jnp.float32)

    return one(ah, bh) + (one(al, bh) + one(ah, bl))


def detect_filters(patch):
    r = REACH
    taps = np.arange(-r, r + 1).astype(np.float32)
    scale = np.float32(2.0 * detect_width * detect_width)
    total = np.sum(np.exp(-taps * taps / scale), dtype=np.float32)
    rows = np.arange(patch, dtype=np.int32)[:, None]
    cols = np.arange(patch + 2 * r, dtype=np.int32)[None, :]
    gap = cols - rows
    inside = (gap >= 0) & (gap <= 2 * r)
    tap = (gap - r).astype(np.float32)
    band = np.where(inside, np.exp(-tap * tap / scale) / total, np.float32(0.0)).astype(np.float32)
    hi = band.astype(jnp.bfloat16)
    lo = (band - hi.astype(np.float32)).astype(jnp.bfloat16)
    mid = np.concatenate([hi[:, r:patch + r], lo[:, r:patch + r]], axis=1)
    edge = np.concatenate([hi[:, :r], hi[:, patch + r:], lo[:, :r], lo[:, patch + r:]], axis=1)
    return jnp.asarray(mid), jnp.asarray(edge)


def detect(coadd, mid, edge):
    ny = lax.axis_size("skyy")
    nx = lax.axis_size("skyx")
    r = REACH
    patch = coadd.shape[0]
    down = [(i, i + 1) for i in range(ny - 1)]
    up = [(i + 1, i) for i in range(ny - 1)]
    right = [(j, j + 1) for j in range(nx - 1)]
    left = [(j + 1, j) for j in range(nx - 1)]
    f32 = jnp.float32
    own = coadd.astype(jnp.bfloat16)
    top = lax.ppermute(own[-r:, :], "skyy", down)
    bottom = lax.ppermute(own[:r, :], "skyy", up)
    vert = jnp.dot(mid, jnp.concatenate([own, own], axis=0), preferred_element_type=f32)
    rim = jnp.concatenate([top, bottom, top, bottom], axis=0)
    vert = vert + jnp.dot(edge, rim, preferred_element_type=f32)
    vown = vert.astype(jnp.bfloat16)
    west = lax.ppermute(vown[:, -r:].T, "skyx", right)
    east = lax.ppermute(vown[:, :r].T, "skyx", left)
    on_cols = (((1,), (1,)), ((), ()))
    by_rows = (((0,), (1,)), ((), ()))
    result = lax.dot_general(
        jnp.concatenate([vown, vown], axis=1), mid, on_cols, preferred_element_type=f32
    )
    side = jnp.concatenate([west, east, west, east], axis=0)
    return result + lax.dot_general(side, edge, by_rows, preferred_element_type=f32)


def body(tiles, coeffs, weights, tile_slot, slot_offset):
    count = tiles.shape[1]
    size = tiles.shape[2]
    columns = lax.axis_size("skyx")
    slots = columns * CAP
    patch = PATCH
    basis = jnp.asarray(band_matrices(size))
    own_tiles = tiles[0]
    own_coeffs = coeffs[0]
    own_weight = weights[0]
    own_slot = tile_slot[0]
    offsets = slot_offset[:, 0, :]
    hits = own_slot[None, :] == jnp.arange(slots, dtype=jnp.int32)[:, None]
    present = jnp.any(hits, axis=1)
    which = jnp.sum(jnp.where(hits, jnp.arange(count, dtype=jnp.int32)[None, :], 0), axis=1)
    which = jnp.where(present, which, count)
    own_matched = match_all(own_tiles, own_coeffs, basis)
    extra = 16
    line = jnp.arange(extra, dtype=jnp.int32)[None, :, None] == 0
    weight_rows = jnp.where(
        line, own_weight[:, None, None], jnp.zeros((), jnp.bfloat16)
    ) * jnp.ones((1, 1, size), jnp.bfloat16)
    carry = jnp.concatenate([own_matched, weight_rows], axis=1)
    carry = jnp.concatenate([carry, jnp.zeros((1, size + extra, size), jnp.bfloat16)], axis=0)
    send = carry[which].reshape(columns, CAP, size + extra, size)
    filters = detect_filters(patch)
    recv = lax.all_to_all(send, "skyx", split_axis=0, concat_axis=0, tiled=True)
    recv, offsets, filters = lax.optimization_barrier((recv, offsets, filters))
    recv = recv.reshape(slots, size + extra, size)
    matched = recv[:, :size, :]
    recv_weight = recv[:, size, 0]
    coadd = coadd_patch(matched, recv_weight, offsets, patch)
    detection = detect(coadd, *filters)
    return (coadd, detection)


def solution(mesh):
    in_specs = (
        P("skyy", "skyx", None, None),
        P("skyy", "skyx", None, None, None),
        P("skyy", "skyx"),
        P("skyy", "skyx"),
        P(None, "skyy", "skyx"),
    )
    out_specs = (P("skyy", "skyx"), P("skyy", "skyx"))
    return jax.shard_map(body, mesh=mesh, in_specs=in_specs, out_specs=out_specs, check_vma=False)
```

```python
import numpy as np
import jax
import jax.numpy as jnp
from jax import lax
from jax.sharding import PartitionSpec as P

REACH = 10
CAP = 2
PATCH = 512


basis_widths = (1.0, 1.8, 2.6, 3.6, 5.0)
detect_width = 2.5


def band_matrices(size):
    rows = np.arange(size, dtype=np.int32)[:, None]
    cols = np.arange(size, dtype=np.int32)[None, :]
    gap = (cols - rows).astype(np.float32)
    inside = np.abs(cols - rows) <= REACH
    taps = np.arange(-REACH, REACH + 1).astype(np.float32)
    mats = []
    for width in basis_widths:
        scale = np.float32(2.0 * width * width)
        total = np.sum(np.exp(-taps * taps / scale), dtype=np.float32)
        mats.append(np.where(inside, np.exp(-gap * gap / scale) / total, np.float32(0.0)))
    return np.stack(mats).astype(np.float32).astype(jnp.bfloat16)


def match_all(tiles, coeffs, basis):
    vert = jnp.einsum(
        "bij,mjk->mbik", basis, tiles, preferred_element_type=jnp.float32
    ).astype(jnp.bfloat16)
    horiz = jnp.einsum("mbik,bjk->mbij", vert, basis, preferred_element_type=jnp.float32)
    return jnp.sum(coeffs.astype(jnp.float32) * horiz, axis=1).astype(jnp.bfloat16)


def coadd_parts(matched, slot_weight, offsets, patch):
    slot_count = matched.shape[0]
    size = matched.shape[1]
    local = jnp.arange(size, dtype=jnp.int32)
    pixel = jnp.arange(patch, dtype=jnp.int32)
    col_hit = offsets[1][:, None, None] + local[None, :, None] == pixel[None, None, :]
    row_hit = offsets[0][None, :, None] + local[None, None, :] == pixel[:, None, None]
    col_place = col_hit.astype(jnp.bfloat16)
    shifted = jnp.einsum(
        "sij,sjq->siq", matched, col_place, preferred_element_type=jnp.float32
    ).astype(jnp.bfloat16)
    zero_weight = jnp.zeros((), jnp.bfloat16)
    row_place = jnp.where(row_hit, slot_weight[None, :, None], zero_weight)
    row_gap = pixel[:, None] - offsets[0][None, :]
    col_gap = pixel[None, :] - offsets[1][:, None]
    row_in = (row_gap >= 0) & (row_gap < size)
    col_in = (col_gap >= 0) & (col_gap < size)
    row_cover = jnp.where(row_in, slot_weight[None, :], zero_weight)
    col_cover = col_in.astype(jnp.bfloat16)
    return (
        row_place.reshape(patch, slot_count * size),
        shifted.reshape(slot_count * size, patch),
        row_cover,
        col_cover,
    )


def coadd_rows(parts, rows):
    row_place, shifted, row_cover, col_cover = parts
    numer = jnp.dot(row_place[rows], shifted, preferred_element_type=jnp.float32)
    cover = jnp.dot(row_cover[rows], col_cover, preferred_element_type=jnp.float32)
    return numer / (1.0 + cover)


def detect_filters(patch):
    r = REACH
    taps = np.arange(-r, r + 1).astype(np.float32)
    scale = np.float32(2.0 * detect_width * detect_width)
    total = np.sum(np.exp(-taps * taps / scale), dtype=np.float32)
    rows = np.arange(patch, dtype=np.int32)[:, None]
    cols = np.arange(patch + 2 * r, dtype=np.int32)[None, :]
    gap = cols - rows
    inside = (gap >= 0) & (gap <= 2 * r)
    tap = (gap - r).astype(np.float32)
    band = np.where(inside, np.exp(-tap * tap / scale) / total, np.float32(0.0)).astype(np.float32)
    hi = band.astype(jnp.bfloat16)
    lo = (band - hi.astype(np.float32)).astype(jnp.bfloat16)
    mid = np.concatenate([hi[:, r:patch + r], lo[:, r:patch + r]], axis=1)
    edge = np.concatenate([hi[:, :r], hi[:, patch + r:], lo[:, :r], lo[:, patch + r:]], axis=1)
    return jnp.asarray(mid), jnp.asarray(edge)


def detect(parts, mid, edge, patch):
    ny = lax.axis_size("skyy")
    nx = lax.axis_size("skyx")
    r = REACH
    down = [(i, i + 1) for i in range(ny - 1)]
    up = [(i + 1, i) for i in range(ny - 1)]
    right = [(j, j + 1) for j in range(nx - 1)]
    left = [(j + 1, j) for j in range(nx - 1)]
    f32 = jnp.float32
    last = coadd_rows(parts, slice(patch - r, patch)).astype(jnp.bfloat16)
    first = coadd_rows(parts, slice(0, r)).astype(jnp.bfloat16)
    top = lax.ppermute(last, "skyy", down)
    bottom = lax.ppermute(first, "skyy", up)
    coadd = coadd_rows(parts, slice(0, patch))
    own = coadd.astype(jnp.bfloat16)
    vert = jnp.dot(mid, jnp.concatenate([own, own], axis=0), preferred_element_type=f32)
    rim = jnp.concatenate([top, bottom, top, bottom], axis=0)
    vert = vert + jnp.dot(edge, rim, preferred_element_type=f32)
    vown = vert.astype(jnp.bfloat16)
    west = lax.ppermute(vown[:, -r:].T, "skyx", right)
    east = lax.ppermute(vown[:, :r].T, "skyx", left)
    on_cols = (((1,), (1,)), ((), ()))
    by_rows = (((0,), (1,)), ((), ()))
    result = lax.dot_general(
        jnp.concatenate([vown, vown], axis=1), mid, on_cols, preferred_element_type=f32
    )
    side = jnp.concatenate([west, east, west, east], axis=0)
    return coadd, result + lax.dot_general(side, edge, by_rows, preferred_element_type=f32)


def body_inner(tiles, coeffs, weights, tile_slot, slot_offset):
    count = tiles.shape[1]
    size = tiles.shape[2]
    columns = lax.axis_size("skyx")
    slots = columns * CAP
    patch = PATCH
    basis = jnp.asarray(band_matrices(size))
    own_tiles = tiles[0]
    own_coeffs = coeffs[0]
    own_weight = weights[0]
    own_slot = tile_slot[0]
    offsets = slot_offset[:, 0, :]
    hits = own_slot[None, :] == jnp.arange(slots, dtype=jnp.int32)[:, None]
    present = jnp.any(hits, axis=1)
    which = jnp.sum(jnp.where(hits, jnp.arange(count, dtype=jnp.int32)[None, :], 0), axis=1)
    which = jnp.where(present, which, count)
    own_matched = match_all(own_tiles, own_coeffs, basis)
    extra = 16
    line = jnp.arange(extra, dtype=jnp.int32)[None, :, None] == 0
    weight_rows = jnp.where(
        line, own_weight[:, None, None], jnp.zeros((), jnp.bfloat16)
    ) * jnp.ones((1, 1, size), jnp.bfloat16)
    carry = jnp.concatenate([own_matched, weight_rows], axis=1)
    carry = jnp.concatenate([carry, jnp.zeros((1, size + extra, size), jnp.bfloat16)], axis=0)
    send = carry[which].reshape(columns, CAP, size + extra, size)
    filters = detect_filters(patch)
    recv = lax.all_to_all(send, "skyx", split_axis=0, concat_axis=0, tiled=True)
    recv, offsets, filters = lax.optimization_barrier((recv, offsets, filters))
    recv = recv.reshape(slots, size + extra, size)
    matched = recv[:, :size, :]
    recv_weight = recv[:, size, 0]
    parts = coadd_parts(matched, recv_weight, offsets, patch)
    coadd, detection = detect(parts, *filters, patch)
    return (coadd, detection)


def solution(mesh):
    in_specs = (
        P("skyy", "skyx", None, None),
        P("skyy", "skyx", None, None, None),
        P("skyy", "skyx"),
        P("skyy", "skyx"),
        P(None, "skyy", "skyx"),
    )
    out_specs = (P("skyy", "skyx"), P("skyy", "skyx"))
    return jax.shard_map(body_inner, mesh=mesh, in_specs=in_specs, out_specs=out_specs, check_vma=False)
```

```python
import numpy as np
import jax
import jax.numpy as jnp
from jax import lax
from jax.sharding import PartitionSpec as P

REACH = 10
CAP = 2
PATCH = 512


basis_widths = (1.0, 1.8, 2.6, 3.6, 5.0)
detect_width = 2.5


def band_matrices(size):
    rows = np.arange(size, dtype=np.int32)[:, None]
    cols = np.arange(size, dtype=np.int32)[None, :]
    gap = (cols - rows).astype(np.float32)
    inside = np.abs(cols - rows) <= REACH
    taps = np.arange(-REACH, REACH + 1).astype(np.float32)
    mats = []
    for width in basis_widths:
        scale = np.float32(2.0 * width * width)
        total = np.sum(np.exp(-taps * taps / scale), dtype=np.float32)
        mats.append(np.where(inside, np.exp(-gap * gap / scale) / total, np.float32(0.0)))
    return np.stack(mats).astype(np.float32).astype(jnp.bfloat16)


def match_all(tiles, coeffs, basis):
    vert = jnp.einsum(
        "bij,mjk->mbik", basis, tiles, preferred_element_type=jnp.float32
    ).astype(jnp.bfloat16)
    horiz = jnp.einsum("mbik,bjk->mbij", vert, basis, preferred_element_type=jnp.float32)
    return jnp.sum(coeffs.astype(jnp.float32) * horiz, axis=1).astype(jnp.bfloat16)


def coadd_patch(matched, slot_weight, offsets, patch):
    slot_count = matched.shape[0]
    size = matched.shape[1]
    local = jnp.arange(size, dtype=jnp.int32)
    pixel = jnp.arange(patch, dtype=jnp.int32)
    col_hit = offsets[1][:, None, None] + local[None, :, None] == pixel[None, None, :]
    row_hit = offsets[0][None, :, None] + local[None, None, :] == pixel[:, None, None]
    col_place = col_hit.astype(jnp.bfloat16)
    shifted = jnp.einsum(
        "sij,sjq->siq", matched, col_place, preferred_element_type=jnp.float32
    ).astype(jnp.bfloat16)
    zero_weight = jnp.zeros((), jnp.bfloat16)
    row_place = jnp.where(row_hit, slot_weight[None, :, None], zero_weight)
    numer = jnp.dot(
        row_place.reshape(patch, slot_count * size),
        shifted.reshape(slot_count * size, patch),
        preferred_element_type=jnp.float32,
    )
    row_gap = pixel[:, None] - offsets[0][None, :]
    col_gap = pixel[None, :] - offsets[1][:, None]
    row_in = (row_gap >= 0) & (row_gap < size)
    col_in = (col_gap >= 0) & (col_gap < size)
    row_cover = jnp.where(row_in, slot_weight[None, :], zero_weight)
    col_cover = col_in.astype(jnp.bfloat16)
    cover = jnp.dot(row_cover, col_cover, preferred_element_type=jnp.float32)
    return numer / (1.0 + cover)


def detect_filters(patch):
    r = REACH
    taps = np.arange(-r, r + 1).astype(np.float32)
    scale = np.float32(2.0 * detect_width * detect_width)
    total = np.sum(np.exp(-taps * taps / scale), dtype=np.float32)
    rows = np.arange(patch, dtype=np.int32)[:, None]
    cols = np.arange(patch + 2 * r, dtype=np.int32)[None, :]
    gap = cols - rows
    inside = (gap >= 0) & (gap <= 2 * r)
    tap = (gap - r).astype(np.float32)
    band = np.where(inside, np.exp(-tap * tap / scale) / total, np.float32(0.0)).astype(np.float32)
    hi = band.astype(jnp.bfloat16)
    lo = (band - hi.astype(np.float32)).astype(jnp.bfloat16)
    mid = np.concatenate([hi[:, r:patch + r], lo[:, r:patch + r]], axis=1)
    edge = np.concatenate([hi[:, :r], hi[:, patch + r:], lo[:, :r], lo[:, patch + r:]], axis=1)
    return jnp.asarray(mid), jnp.asarray(edge)


def detect(coadd, mid, edge):
    ny = lax.axis_size("skyy")
    nx = lax.axis_size("skyx")
    r = REACH
    down = [(i, i + 1) for i in range(ny - 1)]
    up = [(i + 1, i) for i in range(ny - 1)]
    right = [(j, j + 1) for j in range(nx - 1)]
    left = [(j + 1, j) for j in range(nx - 1)]
    f32 = jnp.float32
    own = coadd.astype(jnp.bfloat16)
    top = lax.ppermute(own[-r:, :], "skyy", down)
    bottom = lax.ppermute(own[:r, :], "skyy", up)
    inner = jnp.dot(mid, jnp.concatenate([own, own], axis=0), preferred_element_type=f32)
    inner = lax.optimization_barrier(inner)
    rim = jnp.concatenate([top, bottom, top, bottom], axis=0)
    vert = inner + jnp.dot(edge, rim, preferred_element_type=f32)
    vown = vert.astype(jnp.bfloat16)
    west = lax.ppermute(vown[:, -r:].T, "skyx", right)
    east = lax.ppermute(vown[:, :r].T, "skyx", left)
    on_cols = (((1,), (1,)), ((), ()))
    by_rows = (((0,), (1,)), ((), ()))
    result = lax.dot_general(
        jnp.concatenate([vown, vown], axis=1), mid, on_cols, preferred_element_type=f32
    )
    result = lax.optimization_barrier(result)
    side = jnp.concatenate([west, east, west, east], axis=0)
    return result + lax.dot_general(side, edge, by_rows, preferred_element_type=f32)


def body_inner(tiles, coeffs, weights, tile_slot, slot_offset):
    count = tiles.shape[1]
    size = tiles.shape[2]
    columns = lax.axis_size("skyx")
    slots = columns * CAP
    patch = PATCH
    basis = jnp.asarray(band_matrices(size))
    own_tiles = tiles[0]
    own_coeffs = coeffs[0]
    own_weight = weights[0]
    own_slot = tile_slot[0]
    offsets = slot_offset[:, 0, :]
    hits = own_slot[None, :] == jnp.arange(slots, dtype=jnp.int32)[:, None]
    present = jnp.any(hits, axis=1)
    which = jnp.sum(jnp.where(hits, jnp.arange(count, dtype=jnp.int32)[None, :], 0), axis=1)
    which = jnp.where(present, which, count)
    own_matched = match_all(own_tiles, own_coeffs, basis)
    extra = 16
    line = jnp.arange(extra, dtype=jnp.int32)[None, :, None] == 0
    weight_rows = jnp.where(
        line, own_weight[:, None, None], jnp.zeros((), jnp.bfloat16)
    ) * jnp.ones((1, 1, size), jnp.bfloat16)
    carry = jnp.concatenate([own_matched, weight_rows], axis=1)
    carry = jnp.concatenate([carry, jnp.zeros((1, size + extra, size), jnp.bfloat16)], axis=0)
    send = carry[which].reshape(columns, CAP, size + extra, size)
    filters = detect_filters(patch)
    recv = lax.all_to_all(send, "skyx", split_axis=0, concat_axis=0, tiled=True)
    recv, offsets, filters = lax.optimization_barrier((recv, offsets, filters))
    recv = recv.reshape(slots, size + extra, size)
    matched = recv[:, :size, :]
    recv_weight = recv[:, size, 0]
    coadd = coadd_patch(matched, recv_weight, offsets, patch)
    detection = detect(coadd, *filters)
    return (coadd, detection)


def solution(mesh):
    in_specs = (
        P("skyy", "skyx", None, None),
        P("skyy", "skyx", None, None, None),
        P("skyy", "skyx"),
        P("skyy", "skyx"),
        P(None, "skyy", "skyx"),
    )
    out_specs = (P("skyy", "skyx"), P("skyy", "skyx"))
    return jax.shard_map(body_inner, mesh=mesh, in_specs=in_specs, out_specs=out_specs, check_vma=False)
```

```python
import numpy as np
import jax
import jax.numpy as jnp
from jax import lax
from jax.sharding import PartitionSpec as P

NB = 5
REACH = 10
CAP = 2
PATCH = 512


basis_widths = (1.0, 1.8, 2.6, 3.6, 5.0)
detect_width = 2.5


def band_matrices(size):
    rows = np.arange(size, dtype=np.int32)[:, None]
    cols = np.arange(size, dtype=np.int32)[None, :]
    gap = (cols - rows).astype(np.float32)
    inside = np.abs(cols - rows) <= REACH
    taps = np.arange(-REACH, REACH + 1).astype(np.float32)
    mats = []
    for width in basis_widths:
        scale = np.float32(2.0 * width * width)
        total = np.sum(np.exp(-taps * taps / scale), dtype=np.float32)
        mats.append(np.where(inside, np.exp(-gap * gap / scale) / total, np.float32(0.0)))
    return np.stack(mats).astype(np.float32).astype(jnp.bfloat16)


def match_all(tiles, coeffs, basis):
    vert = jnp.einsum(
        "bij,mjk->mbik", basis, tiles, preferred_element_type=jnp.float32
    ).astype(jnp.bfloat16)
    horiz = jnp.einsum("mbik,bjk->mbij", vert, basis, preferred_element_type=jnp.float32)
    return jnp.sum(coeffs.astype(jnp.float32) * horiz, axis=1).astype(jnp.bfloat16)


def coadd_patch(matched, slot_weight, offsets, patch):
    slot_count = matched.shape[0]
    size = matched.shape[1]
    local = jnp.arange(size, dtype=jnp.int32)
    pixel = jnp.arange(patch, dtype=jnp.int32)
    col_hit = offsets[1][:, None, None] + local[None, :, None] == pixel[None, None, :]
    row_hit = offsets[0][None, :, None] + local[None, None, :] == pixel[:, None, None]
    col_place = col_hit.astype(jnp.bfloat16)
    shifted = jnp.einsum(
        "sij,sjq->siq", matched, col_place, preferred_element_type=jnp.float32
    ).astype(jnp.bfloat16)
    zero_weight = jnp.zeros((), jnp.bfloat16)
    row_place = jnp.where(row_hit, slot_weight[None, :, None], zero_weight)
    numer = jnp.dot(
        row_place.reshape(patch, slot_count * size),
        shifted.reshape(slot_count * size, patch),
        preferred_element_type=jnp.float32,
    )
    row_gap = pixel[:, None] - offsets[0][None, :]
    col_gap = pixel[None, :] - offsets[1][:, None]
    row_in = (row_gap >= 0) & (row_gap < size)
    col_in = (col_gap >= 0) & (col_gap < size)
    row_cover = jnp.where(row_in, slot_weight[None, :], zero_weight)
    col_cover = col_in.astype(jnp.bfloat16)
    cover = jnp.dot(row_cover, col_cover, preferred_element_type=jnp.float32)
    return numer / (1.0 + cover)


def split(x):
    hi = lax.reduce_precision(x, exponent_bits=8, mantissa_bits=7)
    return hi.astype(jnp.bfloat16), (x - hi).astype(jnp.bfloat16)


def mm3(a, b, dims=(((1,), (0,)), ((), ()))):
    ah, al = a
    bh, bl = b

    def one(x, y):
        return lax.dot_general(x, y, dims, preferred_element_type=jnp.float32)

    return one(ah, bh) + (one(al, bh) + one(ah, bl))


def detect_filters(patch):
    r = REACH
    taps = np.arange(-r, r + 1).astype(np.float32)
    scale = np.float32(2.0 * detect_width * detect_width)
    total = np.sum(np.exp(-taps * taps / scale), dtype=np.float32)
    rows = np.arange(patch, dtype=np.int32)[:, None]
    cols = np.arange(patch + 2 * r, dtype=np.int32)[None, :]
    gap = cols - rows
    inside = (gap >= 0) & (gap <= 2 * r)
    tap = (gap - r).astype(np.float32)
    band = np.where(inside, np.exp(-tap * tap / scale) / total, np.float32(0.0)).astype(np.float32)
    hi = band.astype(jnp.bfloat16)
    lo = (band - hi.astype(np.float32)).astype(jnp.bfloat16)
    mid = np.concatenate([hi[:, r:patch + r], lo[:, r:patch + r]], axis=1)
    edge = np.concatenate([hi[:, :r], hi[:, patch + r:], lo[:, :r], lo[:, patch + r:]], axis=1)
    return jnp.asarray(mid), jnp.asarray(edge)


def detect(coadd, mid, edge):
    ny = lax.axis_size("skyy")
    nx = lax.axis_size("skyx")
    r = REACH
    patch = coadd.shape[0]
    down = [(i, i + 1) for i in range(ny - 1)]
    up = [(i + 1, i) for i in range(ny - 1)]
    right = [(j, j + 1) for j in range(nx - 1)]
    left = [(j + 1, j) for j in range(nx - 1)]
    f32 = jnp.float32
    own = coadd.astype(jnp.bfloat16)
    west = lax.ppermute(own[:, -r:].T, "skyx", right)
    east = lax.ppermute(own[:, :r].T, "skyx", left)
    on_cols = (((1,), (1,)), ((), ()))
    by_rows = (((0,), (1,)), ((), ()))
    horiz = lax.dot_general(
        jnp.concatenate([own, own], axis=1), mid, on_cols, preferred_element_type=f32
    )
    side = jnp.concatenate([west, east, west, east], axis=0)
    horiz = horiz + lax.dot_general(side, edge, by_rows, preferred_element_type=f32)
    hown = horiz.astype(jnp.bfloat16)
    top = lax.ppermute(hown[-r:, :], "skyy", down)
    bottom = lax.ppermute(hown[:r, :], "skyy", up)
    result = jnp.dot(mid, jnp.concatenate([hown, hown], axis=0), preferred_element_type=f32)
    rim = jnp.concatenate([top, bottom, top, bottom], axis=0)
    return result + jnp.dot(edge, rim, preferred_element_type=f32)


def body(tiles, coeffs, weights, tile_slot, slot_offset):
    count = tiles.shape[1]
    size = tiles.shape[2]
    columns = lax.axis_size("skyx")
    slots = columns * CAP
    patch = PATCH
    basis = jnp.asarray(band_matrices(size))
    own_tiles = tiles[0]
    own_coeffs = coeffs[0]
    own_weight = weights[0]
    own_slot = tile_slot[0]
    offsets = slot_offset[:, 0, :]
    hits = own_slot[None, :] == jnp.arange(slots, dtype=jnp.int32)[:, None]
    present = jnp.any(hits, axis=1)
    which = jnp.sum(jnp.where(hits, jnp.arange(count, dtype=jnp.int32)[None, :], 0), axis=1)
    which = jnp.where(present, which, count)
    own_matched = match_all(own_tiles, own_coeffs, basis)
    extra = 16
    line = jnp.arange(extra, dtype=jnp.int32)[None, :, None] == 0
    weight_rows = jnp.where(
        line, own_weight[:, None, None], jnp.zeros((), jnp.bfloat16)
    ) * jnp.ones((1, 1, size), jnp.bfloat16)
    carry = jnp.concatenate([own_matched, weight_rows], axis=1)
    carry = jnp.concatenate([carry, jnp.zeros((1, size + extra, size), jnp.bfloat16)], axis=0)
    send = carry[which].reshape(columns, CAP, size + extra, size)
    filters = detect_filters(patch)
    recv = lax.all_to_all(send, "skyx", split_axis=0, concat_axis=0, tiled=True)
    recv, offsets, filters = lax.optimization_barrier((recv, offsets, filters))
    recv = recv.reshape(slots, size + extra, size)
    matched = recv[:, :size, :]
    recv_weight = recv[:, size, 0]
    coadd = coadd_patch(matched, recv_weight, offsets, patch)
    detection = detect(coadd, *filters)
    return (coadd, detection)


def solution(mesh):
    in_specs = (
        P("skyy", "skyx", None, None),
        P("skyy", "skyx", None, None, None),
        P("skyy", "skyx"),
        P("skyy", "skyx"),
        P(None, "skyy", "skyx"),
    )
    out_specs = (P("skyy", "skyx"), P("skyy", "skyx"))
    return jax.shard_map(body, mesh=mesh, in_specs=in_specs, out_specs=out_specs, check_vma=False)
```

```python
import numpy as np
import jax
import jax.numpy as jnp
from jax import lax
from jax.sharding import PartitionSpec as P

NB = 5
REACH = 10
CAP = 2
PATCH = 512


basis_widths = (1.0, 1.8, 2.6, 3.6, 5.0)
detect_width = 2.5


def band_matrices(size):
    rows = np.arange(size, dtype=np.int32)[:, None]
    cols = np.arange(size, dtype=np.int32)[None, :]
    gap = (cols - rows).astype(np.float32)
    inside = np.abs(cols - rows) <= REACH
    taps = np.arange(-REACH, REACH + 1).astype(np.float32)
    mats = []
    for width in basis_widths:
        scale = np.float32(2.0 * width * width)
        total = np.sum(np.exp(-taps * taps / scale), dtype=np.float32)
        mats.append(np.where(inside, np.exp(-gap * gap / scale) / total, np.float32(0.0)))
    return np.stack(mats).astype(np.float32).astype(jnp.bfloat16)


def match_all(tiles, coeffs, basis):
    vert = jnp.einsum(
        "bij,mjk->mbik", basis, tiles, preferred_element_type=jnp.float32
    ).astype(jnp.bfloat16)
    horiz = jnp.einsum("mbik,bjk->mbij", vert, basis, preferred_element_type=jnp.float32)
    return jnp.sum(coeffs.astype(jnp.float32) * horiz, axis=1).astype(jnp.bfloat16)


def coadd_patch(matched, slot_weight, offsets, patch):
    slot_count = matched.shape[0]
    size = matched.shape[1]
    local = jnp.arange(size, dtype=jnp.int32)
    pixel = jnp.arange(patch, dtype=jnp.int32)
    col_hit = offsets[1][:, None, None] + local[None, :, None] == pixel[None, None, :]
    row_hit = offsets[0][None, :, None] + local[None, None, :] == pixel[:, None, None]
    col_place = col_hit.astype(jnp.bfloat16)
    shifted = jnp.einsum(
        "sij,sjq->siq", matched, col_place, preferred_element_type=jnp.float32
    ).astype(jnp.bfloat16)
    zero_weight = jnp.zeros((), jnp.bfloat16)
    row_place = jnp.where(row_hit, slot_weight[None, :, None], zero_weight)
    numer = jnp.dot(
        row_place.reshape(patch, slot_count * size),
        shifted.reshape(slot_count * size, patch),
        preferred_element_type=jnp.float32,
    )
    row_gap = pixel[:, None] - offsets[0][None, :]
    col_gap = pixel[None, :] - offsets[1][:, None]
    row_in = (row_gap >= 0) & (row_gap < size)
    col_in = (col_gap >= 0) & (col_gap < size)
    row_cover = jnp.where(row_in, slot_weight[None, :], zero_weight)
    col_cover = col_in.astype(jnp.bfloat16)
    cover = jnp.dot(row_cover, col_cover, preferred_element_type=jnp.float32)
    return numer / (1.0 + cover)


def split(x):
    hi = lax.reduce_precision(x, exponent_bits=8, mantissa_bits=7)
    return hi.astype(jnp.bfloat16), (x - hi).astype(jnp.bfloat16)


def mm3(a, b, dims=(((1,), (0,)), ((), ()))):
    ah, al = a
    bh, bl = b

    def one(x, y):
        return lax.dot_general(x, y, dims, preferred_element_type=jnp.float32)

    return one(ah, bh) + (one(al, bh) + one(ah, bl))


def detect_filters(patch):
    r = REACH
    taps = np.arange(-r, r + 1).astype(np.float32)
    scale = np.float32(2.0 * detect_width * detect_width)
    total = np.sum(np.exp(-taps * taps / scale), dtype=np.float32)
    rows = np.arange(patch, dtype=np.int32)[:, None]
    cols = np.arange(patch + 2 * r, dtype=np.int32)[None, :]
    gap = cols - rows
    inside = (gap >= 0) & (gap <= 2 * r)
    tap = (gap - r).astype(np.float32)
    band = np.where(inside, np.exp(-tap * tap / scale) / total, np.float32(0.0)).astype(np.float32)
    hi = band.astype(jnp.bfloat16)
    lo = (band - hi.astype(np.float32)).astype(jnp.bfloat16)
    mid = np.concatenate([hi[:, r:patch + r], lo[:, r:patch + r]], axis=1)
    edge = np.concatenate([hi[:, :r], hi[:, patch + r:], lo[:, :r], lo[:, patch + r:]], axis=1)
    return jnp.asarray(mid), jnp.asarray(edge)


def detect(coadd, mid, edge):
    ny = lax.axis_size("skyy")
    nx = lax.axis_size("skyx")
    r = REACH
    patch = coadd.shape[0]
    down = [(i, i + 1) for i in range(ny - 1)]
    up = [(i + 1, i) for i in range(ny - 1)]
    right = [(j, j + 1) for j in range(nx - 1)]
    left = [(j + 1, j) for j in range(nx - 1)]
    f32 = jnp.float32
    own = coadd.astype(jnp.bfloat16)
    top = lax.ppermute(own[-r:, :], "skyy", down)
    bottom = lax.ppermute(own[:r, :], "skyy", up)
    vert = jnp.dot(mid, jnp.concatenate([own, own], axis=0), preferred_element_type=f32)
    rim = jnp.concatenate([top, bottom, top, bottom], axis=0)
    vert = vert + jnp.dot(edge, rim, preferred_element_type=f32)
    vown = vert.astype(jnp.bfloat16)
    west = lax.ppermute(vown[:, -r:].T, "skyx", right)
    east = lax.ppermute(vown[:, :r].T, "skyx", left)
    on_cols = (((1,), (1,)), ((), ()))
    by_rows = (((0,), (1,)), ((), ()))
    result = lax.dot_general(
        jnp.concatenate([vown, vown], axis=1), mid, on_cols, preferred_element_type=f32
    )
    side = jnp.concatenate([west, east, west, east], axis=0)
    return result + lax.dot_general(side, edge, by_rows, preferred_element_type=f32)


def body(tiles, coeffs, weights, tile_slot, slot_offset):
    count = tiles.shape[1]
    size = tiles.shape[2]
    columns = lax.axis_size("skyx")
    slots = columns * CAP
    patch = PATCH
    basis = jnp.asarray(band_matrices(size))
    own_tiles = tiles[0]
    own_coeffs = coeffs[0]
    own_weight = weights[0]
    own_slot = tile_slot[0]
    offsets = slot_offset[:, 0, :]
    which = jnp.full((slots,), count, jnp.int32).at[own_slot].set(
        jnp.arange(count, dtype=jnp.int32), unique_indices=True, mode="promise_in_bounds"
    )
    own_matched = match_all(own_tiles, own_coeffs, basis)
    extra = 16
    line = jnp.arange(extra, dtype=jnp.int32)[None, :, None] == 0
    weight_rows = jnp.where(
        line, own_weight[:, None, None], jnp.zeros((), jnp.bfloat16)
    ) * jnp.ones((1, 1, size), jnp.bfloat16)
    carry = jnp.concatenate([own_matched, weight_rows], axis=1)
    carry = jnp.concatenate([carry, jnp.zeros((1, size + extra, size), jnp.bfloat16)], axis=0)
    send = carry[which].reshape(columns, CAP, size + extra, size)
    filters = detect_filters(patch)
    recv = lax.all_to_all(send, "skyx", split_axis=0, concat_axis=0, tiled=True)
    recv, offsets, filters = lax.optimization_barrier((recv, offsets, filters))
    recv = recv.reshape(slots, size + extra, size)
    matched = recv[:, :size, :]
    recv_weight = recv[:, size, 0]
    coadd = coadd_patch(matched, recv_weight, offsets, patch)
    detection = detect(coadd, *filters)
    return (coadd, detection)


def solution(mesh):
    in_specs = (
        P("skyy", "skyx", None, None),
        P("skyy", "skyx", None, None, None),
        P("skyy", "skyx"),
        P("skyy", "skyx"),
        P(None, "skyy", "skyx"),
    )
    out_specs = (P("skyy", "skyx"), P("skyy", "skyx"))
    return jax.shard_map(body, mesh=mesh, in_specs=in_specs, out_specs=out_specs, check_vma=False)
```

```python
import numpy as np
import jax
import jax.numpy as jnp
from jax import lax
from jax.sharding import PartitionSpec as P

NB = 5
REACH = 10
CAP = 2
PATCH = 512


basis_widths = (1.0, 1.8, 2.6, 3.6, 5.0)
detect_width = 2.5


def band_matrices(size):
    rows = np.arange(size, dtype=np.int32)[:, None]
    cols = np.arange(size, dtype=np.int32)[None, :]
    gap = (cols - rows).astype(np.float32)
    inside = np.abs(cols - rows) <= REACH
    taps = np.arange(-REACH, REACH + 1).astype(np.float32)
    mats = []
    for width in basis_widths:
        scale = np.float32(2.0 * width * width)
        total = np.sum(np.exp(-taps * taps / scale), dtype=np.float32)
        mats.append(np.where(inside, np.exp(-gap * gap / scale) / total, np.float32(0.0)))
    return np.stack(mats).astype(np.float32).astype(jnp.bfloat16)


def match_all(tiles, coeffs, basis):
    vert = jnp.einsum(
        "bij,mjk->mbik", basis, tiles, preferred_element_type=jnp.float32
    ).astype(jnp.bfloat16)
    horiz = jnp.einsum("mbik,bjk->mbij", vert, basis, preferred_element_type=jnp.float32)
    return jnp.sum(coeffs.astype(jnp.float32) * horiz, axis=1).astype(jnp.bfloat16)


def coadd_patch(matched, slot_weight, offsets, patch):
    slot_count = matched.shape[0]
    size = matched.shape[1]
    local = jnp.arange(size, dtype=jnp.int32)
    pixel = jnp.arange(patch, dtype=jnp.int32)
    col_hit = offsets[1][:, None, None] + local[None, :, None] == pixel[None, None, :]
    row_hit = offsets[0][None, :, None] + local[None, None, :] == pixel[:, None, None]
    col_place = col_hit.astype(jnp.bfloat16)
    shifted = jnp.einsum(
        "sij,sjq->siq", matched, col_place, preferred_element_type=jnp.float32
    ).astype(jnp.bfloat16)
    zero_weight = jnp.zeros((), jnp.bfloat16)
    row_place = jnp.where(row_hit, slot_weight[None, :, None], zero_weight)
    numer = jnp.dot(
        row_place.reshape(patch, slot_count * size),
        shifted.reshape(slot_count * size, patch),
        preferred_element_type=jnp.float32,
    )
    row_gap = pixel[:, None] - offsets[0][None, :]
    col_gap = pixel[None, :] - offsets[1][:, None]
    row_in = (row_gap >= 0) & (row_gap < size)
    col_in = (col_gap >= 0) & (col_gap < size)
    row_cover = jnp.where(row_in, slot_weight[None, :], zero_weight)
    col_cover = col_in.astype(jnp.bfloat16)
    cover = jnp.dot(row_cover, col_cover, preferred_element_type=jnp.float32)
    return numer / (1.0 + cover)


def split(x):
    hi = lax.reduce_precision(x, exponent_bits=8, mantissa_bits=7)
    return hi.astype(jnp.bfloat16), (x - hi).astype(jnp.bfloat16)


def mm3(a, b, dims=(((1,), (0,)), ((), ()))):
    ah, al = a
    bh, bl = b

    def one(x, y):
        return lax.dot_general(x, y, dims, preferred_element_type=jnp.float32)

    return one(ah, bh) + (one(al, bh) + one(ah, bl))


def detect_filters(patch):
    r = REACH
    taps = np.arange(-r, r + 1).astype(np.float32)
    scale = np.float32(2.0 * detect_width * detect_width)
    total = np.sum(np.exp(-taps * taps / scale), dtype=np.float32)
    rows = np.arange(patch, dtype=np.int32)[:, None]
    cols = np.arange(patch + 2 * r, dtype=np.int32)[None, :]
    gap = cols - rows
    inside = (gap >= 0) & (gap <= 2 * r)
    tap = (gap - r).astype(np.float32)
    band = np.where(inside, np.exp(-tap * tap / scale) / total, np.float32(0.0)).astype(np.float32)
    hi = band.astype(jnp.bfloat16)
    lo = (band - hi.astype(np.float32)).astype(jnp.bfloat16)
    mid = np.concatenate([hi[:, r:patch + r], lo[:, r:patch + r]], axis=1)
    edge = np.concatenate([hi[:, :r], hi[:, patch + r:], lo[:, :r], lo[:, patch + r:]], axis=1)
    return jnp.asarray(mid), jnp.asarray(edge)


def detect(coadd, mid, edge):
    ny = lax.axis_size("skyy")
    nx = lax.axis_size("skyx")
    r = REACH
    patch = coadd.shape[0]
    down = [(i, i + 1) for i in range(ny - 1)]
    up = [(i + 1, i) for i in range(ny - 1)]
    right = [(j, j + 1) for j in range(nx - 1)]
    left = [(j + 1, j) for j in range(nx - 1)]
    f32 = jnp.float32
    own = coadd.astype(jnp.bfloat16)
    top = lax.ppermute(own[-r:, :], "skyy", down)
    bottom = lax.ppermute(own[:r, :], "skyy", up)
    vert = jnp.dot(mid, jnp.concatenate([own, own], axis=0), preferred_element_type=f32)
    rim = jnp.concatenate([top, bottom, top, bottom], axis=0)
    vert = vert + jnp.dot(edge, rim, preferred_element_type=f32)
    vown = vert.astype(jnp.bfloat16)
    west = lax.ppermute(vown[:, -r:].T, "skyx", right)
    east = lax.ppermute(vown[:, :r].T, "skyx", left)
    on_cols = (((1,), (1,)), ((), ()))
    by_rows = (((0,), (1,)), ((), ()))
    result = lax.dot_general(
        jnp.concatenate([vown, vown], axis=1), mid, on_cols, preferred_element_type=f32
    )
    side = jnp.concatenate([west, east, west, east], axis=0)
    return result + lax.dot_general(side, edge, by_rows, preferred_element_type=f32)


def body(tiles, coeffs, weights, tile_slot, slot_offset):
    count = tiles.shape[1]
    size = tiles.shape[2]
    columns = lax.axis_size("skyx")
    slots = columns * CAP
    patch = PATCH
    basis = jnp.asarray(band_matrices(size))
    own_tiles = tiles[0]
    own_coeffs = coeffs[0]
    own_weight = weights[0]
    own_slot = tile_slot[0]
    offsets = slot_offset[:, 0, :]
    hits = own_slot[None, :] == jnp.arange(slots, dtype=jnp.int32)[:, None]
    present = jnp.any(hits, axis=1)
    which = jnp.sum(jnp.where(hits, jnp.arange(count, dtype=jnp.int32)[None, :], 0), axis=1)
    which = jnp.where(present, which, count)
    own_matched = match_all(own_tiles, own_coeffs, basis)
    extra = 16
    weight_rows = jnp.broadcast_to(own_weight[:, None, None], (count, extra, size))
    carry = jnp.concatenate([own_matched, weight_rows], axis=1)
    carry = jnp.concatenate([carry, jnp.zeros((1, size + extra, size), jnp.bfloat16)], axis=0)
    send = carry[which].reshape(columns, CAP, size + extra, size)
    filters = detect_filters(patch)
    recv = lax.all_to_all(send, "skyx", split_axis=0, concat_axis=0, tiled=True)
    recv, offsets, filters = lax.optimization_barrier((recv, offsets, filters))
    recv = recv.reshape(slots, size + extra, size)
    matched = recv[:, :size, :]
    recv_weight = recv[:, size, 0]
    coadd = coadd_patch(matched, recv_weight, offsets, patch)
    detection = detect(coadd, *filters)
    return (coadd, detection)


def solution(mesh):
    in_specs = (
        P("skyy", "skyx", None, None),
        P("skyy", "skyx", None, None, None),
        P("skyy", "skyx"),
        P("skyy", "skyx"),
        P(None, "skyy", "skyx"),
    )
    out_specs = (P("skyy", "skyx"), P("skyy", "skyx"))
    return jax.shard_map(body, mesh=mesh, in_specs=in_specs, out_specs=out_specs, check_vma=False)
```

```python
import numpy as np
import jax
import jax.numpy as jnp
from jax import lax
from jax.sharding import PartitionSpec as P

NB = 5
REACH = 10
CAP = 2
PATCH = 512


basis_widths = (1.0, 1.8, 2.6, 3.6, 5.0)
detect_width = 2.5


def band_matrices(size):
    rows = np.arange(size, dtype=np.int32)[:, None]
    cols = np.arange(size, dtype=np.int32)[None, :]
    gap = (cols - rows).astype(np.float32)
    inside = np.abs(cols - rows) <= REACH
    taps = np.arange(-REACH, REACH + 1).astype(np.float32)
    mats = []
    for width in basis_widths:
        scale = np.float32(2.0 * width * width)
        total = np.sum(np.exp(-taps * taps / scale), dtype=np.float32)
        mats.append(np.where(inside, np.exp(-gap * gap / scale) / total, np.float32(0.0)))
    return np.stack(mats).astype(np.float32).astype(jnp.bfloat16)


def match_all(tiles, coeffs, basis):
    vert = jnp.einsum(
        "bij,mjk->mbik", basis, tiles, preferred_element_type=jnp.float32
    ).astype(jnp.bfloat16)
    horiz = jnp.einsum("mbik,bjk->mbij", vert, basis, preferred_element_type=jnp.float32)
    return jnp.sum(coeffs.astype(jnp.float32) * horiz, axis=1).astype(jnp.bfloat16)


def coadd_patch(matched, slot_weight, offsets, patch):
    slot_count = matched.shape[0]
    size = matched.shape[1]
    local = jnp.arange(size, dtype=jnp.int32)
    pixel = jnp.arange(patch, dtype=jnp.int32)
    col_hit = offsets[1][:, None, None] + local[None, :, None] == pixel[None, None, :]
    row_hit = offsets[0][None, :, None] + local[None, None, :] == pixel[:, None, None]
    col_place = col_hit.astype(jnp.bfloat16)
    shifted = jnp.einsum(
        "sij,sjq->siq", matched, col_place, preferred_element_type=jnp.float32
    ).astype(jnp.bfloat16)
    zero_weight = jnp.zeros((), jnp.bfloat16)
    row_place = jnp.where(row_hit, slot_weight[None, :, None], zero_weight)
    numer = jnp.dot(
        row_place.reshape(patch, slot_count * size),
        shifted.reshape(slot_count * size, patch),
        preferred_element_type=jnp.float32,
    )
    row_gap = pixel[:, None] - offsets[0][None, :]
    col_gap = pixel[None, :] - offsets[1][:, None]
    row_in = (row_gap >= 0) & (row_gap < size)
    col_in = (col_gap >= 0) & (col_gap < size)
    row_cover = jnp.where(row_in, slot_weight[None, :], zero_weight)
    col_cover = col_in.astype(jnp.bfloat16)
    cover = jnp.dot(row_cover, col_cover, preferred_element_type=jnp.float32)
    return numer / (1.0 + cover)


def split(x):
    hi = lax.reduce_precision(x, exponent_bits=8, mantissa_bits=7)
    return hi.astype(jnp.bfloat16), (x - hi).astype(jnp.bfloat16)


def mm3(a, b, dims=(((1,), (0,)), ((), ()))):
    ah, al = a
    bh, bl = b

    def one(x, y):
        return lax.dot_general(x, y, dims, preferred_element_type=jnp.float32)

    return one(ah, bh) + (one(al, bh) + one(ah, bl))


def detect_filters(patch):
    r = REACH
    taps = np.arange(-r, r + 1).astype(np.float32)
    scale = np.float32(2.0 * detect_width * detect_width)
    total = np.sum(np.exp(-taps * taps / scale), dtype=np.float32)
    rows = np.arange(patch, dtype=np.int32)[:, None]
    cols = np.arange(patch + 2 * r, dtype=np.int32)[None, :]
    gap = cols - rows
    inside = (gap >= 0) & (gap <= 2 * r)
    tap = (gap - r).astype(np.float32)
    band = np.where(inside, np.exp(-tap * tap / scale) / total, np.float32(0.0)).astype(np.float32)
    hi = band.astype(jnp.bfloat16)
    lo = (band - hi.astype(np.float32)).astype(jnp.bfloat16)
    mid = np.concatenate([hi[:, r:patch + r], lo[:, r:patch + r]], axis=1)
    edge = np.concatenate([hi[:, :r], hi[:, patch + r:], lo[:, :r], lo[:, patch + r:]], axis=1)
    return jnp.asarray(mid), jnp.asarray(edge)


def detect(coadd, mid, edge):
    ny = lax.axis_size("skyy")
    nx = lax.axis_size("skyx")
    r = REACH
    patch = coadd.shape[0]
    down = [(i, i + 1) for i in range(ny - 1)]
    up = [(i + 1, i) for i in range(ny - 1)]
    right = [(j, j + 1) for j in range(nx - 1)]
    left = [(j + 1, j) for j in range(nx - 1)]
    f32 = jnp.float32
    own = coadd.astype(jnp.bfloat16)
    top = lax.ppermute(own[-r:, :], "skyy", down)
    bottom = lax.ppermute(own[:r, :], "skyy", up)
    vert = jnp.dot(mid, jnp.concatenate([own, own], axis=0), preferred_element_type=f32)
    rim = jnp.concatenate([top, bottom, top, bottom], axis=0)
    vert = vert + jnp.dot(edge, rim, preferred_element_type=f32)
    vown = vert.astype(jnp.bfloat16)
    west = lax.ppermute(vown[:, -r:].T, "skyx", right)
    east = lax.ppermute(vown[:, :r].T, "skyx", left)
    on_cols = (((1,), (1,)), ((), ()))
    by_rows = (((0,), (1,)), ((), ()))
    result = lax.dot_general(
        jnp.concatenate([vown, vown], axis=1), mid, on_cols, preferred_element_type=f32
    )
    side = jnp.concatenate([west, east, west, east], axis=0)
    return result + lax.dot_general(side, edge, by_rows, preferred_element_type=f32)


def body(tiles, coeffs, weights, tile_slot, slot_offset):
    count = tiles.shape[1]
    size = tiles.shape[2]
    columns = lax.axis_size("skyx")
    slots = columns * CAP
    patch = PATCH
    basis = jnp.asarray(band_matrices(size))
    own_tiles = tiles[0]
    own_coeffs = coeffs[0]
    own_weight = weights[0]
    own_slot = tile_slot[0]
    offsets = slot_offset[:, 0, :]
    which = jnp.full((slots,), count, jnp.int32).at[own_slot].set(
        jnp.arange(count, dtype=jnp.int32), unique_indices=True, mode="promise_in_bounds"
    )
    own_matched = match_all(own_tiles, own_coeffs, basis)
    extra = 16
    weight_rows = jnp.broadcast_to(own_weight[:, None, None], (count, extra, size))
    carry = jnp.concatenate([own_matched, weight_rows], axis=1)
    carry = jnp.concatenate([carry, jnp.zeros((1, size + extra, size), jnp.bfloat16)], axis=0)
    send = carry[which].reshape(columns, CAP, size + extra, size)
    filters = detect_filters(patch)
    recv = lax.all_to_all(send, "skyx", split_axis=0, concat_axis=0, tiled=True)
    recv, offsets, filters = lax.optimization_barrier((recv, offsets, filters))
    recv = recv.reshape(slots, size + extra, size)
    matched = recv[:, :size, :]
    recv_weight = recv[:, size, 0]
    coadd = coadd_patch(matched, recv_weight, offsets, patch)
    detection = detect(coadd, *filters)
    return (coadd, detection)


def solution(mesh):
    in_specs = (
        P("skyy", "skyx", None, None),
        P("skyy", "skyx", None, None, None),
        P("skyy", "skyx"),
        P("skyy", "skyx"),
        P(None, "skyy", "skyx"),
    )
    out_specs = (P("skyy", "skyx"), P("skyy", "skyx"))
    return jax.shard_map(body, mesh=mesh, in_specs=in_specs, out_specs=out_specs, check_vma=False)
```

```python
import numpy as np
import jax
import jax.numpy as jnp
from jax import lax
from jax.sharding import PartitionSpec as P

NB = 5
REACH = 10
CAP = 2
PATCH = 512


basis_widths = (1.0, 1.8, 2.6, 3.6, 5.0)
detect_width = 2.5


def band_matrices(size):
    rows = np.arange(size, dtype=np.int32)[:, None]
    cols = np.arange(size, dtype=np.int32)[None, :]
    gap = (cols - rows).astype(np.float32)
    inside = np.abs(cols - rows) <= REACH
    taps = np.arange(-REACH, REACH + 1).astype(np.float32)
    mats = []
    for width in basis_widths:
        scale = np.float32(2.0 * width * width)
        total = np.sum(np.exp(-taps * taps / scale), dtype=np.float32)
        mats.append(np.where(inside, np.exp(-gap * gap / scale) / total, np.float32(0.0)))
    return np.stack(mats).astype(np.float32).astype(jnp.bfloat16)


def match_all(tiles, coeffs, basis):
    vert = jnp.einsum(
        "bij,mjk->mbik", basis, tiles, preferred_element_type=jnp.float32
    ).astype(jnp.bfloat16)
    horiz = jnp.einsum("mbik,bjk->mbij", vert, basis, preferred_element_type=jnp.float32)
    return jnp.sum(coeffs.astype(jnp.float32) * horiz, axis=1).astype(jnp.bfloat16)


def coadd_patch(matched, slot_weight, offsets, patch):
    slot_count = matched.shape[0]
    size = matched.shape[1]
    local = jnp.arange(size, dtype=jnp.int32)
    pixel = jnp.arange(patch, dtype=jnp.int32)
    col_hit = offsets[1][:, None, None] + local[None, :, None] == pixel[None, None, :]
    row_hit = offsets[0][None, :, None] + local[None, None, :] == pixel[:, None, None]
    col_place = col_hit.astype(jnp.bfloat16)
    shifted = jnp.einsum(
        "sij,sjq->siq", matched, col_place, preferred_element_type=jnp.float32
    ).astype(jnp.bfloat16)
    zero_weight = jnp.zeros((), jnp.bfloat16)
    row_place = jnp.where(row_hit, slot_weight[None, :, None], zero_weight)
    numer = jnp.dot(
        row_place.reshape(patch, slot_count * size),
        shifted.reshape(slot_count * size, patch),
        preferred_element_type=jnp.float32,
    )
    row_gap = pixel[:, None] - offsets[0][None, :]
    col_gap = pixel[None, :] - offsets[1][:, None]
    row_in = (row_gap >= 0) & (row_gap < size)
    col_in = (col_gap >= 0) & (col_gap < size)
    row_cover = jnp.where(row_in, slot_weight[None, :], zero_weight)
    col_cover = col_in.astype(jnp.bfloat16)
    cover = jnp.dot(row_cover, col_cover, preferred_element_type=jnp.float32)
    return numer / (1.0 + cover)


def split(x):
    hi = lax.reduce_precision(x, exponent_bits=8, mantissa_bits=7)
    return hi.astype(jnp.bfloat16), (x - hi).astype(jnp.bfloat16)


def mm3(a, b, dims=(((1,), (0,)), ((), ()))):
    ah, al = a
    bh, bl = b

    def one(x, y):
        return lax.dot_general(x, y, dims, preferred_element_type=jnp.float32)

    return one(ah, bh) + (one(al, bh) + one(ah, bl))


def detect_filters(patch):
    r = REACH
    taps = np.arange(-r, r + 1).astype(np.float32)
    scale = np.float32(2.0 * detect_width * detect_width)
    total = np.sum(np.exp(-taps * taps / scale), dtype=np.float32)
    rows = np.arange(patch, dtype=np.int32)[:, None]
    cols = np.arange(patch + 2 * r, dtype=np.int32)[None, :]
    gap = cols - rows
    inside = (gap >= 0) & (gap <= 2 * r)
    tap = (gap - r).astype(np.float32)
    band = np.where(inside, np.exp(-tap * tap / scale) / total, np.float32(0.0)).astype(np.float32)
    hi = band.astype(jnp.bfloat16)
    lo = (band - hi.astype(np.float32)).astype(jnp.bfloat16)
    mid = np.concatenate([hi[:, r:patch + r], lo[:, r:patch + r]], axis=1)
    edge = np.concatenate([hi[:, :r], hi[:, patch + r:], lo[:, :r], lo[:, patch + r:]], axis=1)
    return jnp.asarray(mid), jnp.asarray(edge)


def detect(coadd, mid, edge):
    ny = lax.axis_size("skyy")
    nx = lax.axis_size("skyx")
    r = REACH
    patch = coadd.shape[0]
    down = [(i, i + 1) for i in range(ny - 1)]
    up = [(i + 1, i) for i in range(ny - 1)]
    right = [(j, j + 1) for j in range(nx - 1)]
    left = [(j + 1, j) for j in range(nx - 1)]
    f32 = jnp.float32
    own = coadd.astype(jnp.bfloat16)
    top = lax.ppermute(own[-r:, :], "skyy", down)
    bottom = lax.ppermute(own[:r, :], "skyy", up)
    vert = jnp.dot(mid, jnp.concatenate([own, own], axis=0), preferred_element_type=f32)
    rim = jnp.concatenate([top, bottom, top, bottom], axis=0)
    vert = vert + jnp.dot(edge, rim, preferred_element_type=f32)
    vown = vert.astype(jnp.bfloat16)
    west = lax.ppermute(vown[:, -r:].T, "skyx", right)
    east = lax.ppermute(vown[:, :r].T, "skyx", left)
    on_cols = (((1,), (1,)), ((), ()))
    by_rows = (((0,), (1,)), ((), ()))
    result = lax.dot_general(
        jnp.concatenate([vown, vown], axis=1), mid, on_cols, preferred_element_type=f32
    )
    side = jnp.concatenate([west, east, west, east], axis=0)
    return result + lax.dot_general(side, edge, by_rows, preferred_element_type=f32)


def body(tiles, coeffs, weights, tile_slot, slot_offset):
    count = tiles.shape[1]
    size = tiles.shape[2]
    columns = lax.axis_size("skyx")
    slots = columns * CAP
    patch = PATCH
    basis = jnp.asarray(band_matrices(size))
    own_tiles = tiles[0]
    own_coeffs = coeffs[0]
    own_weight = weights[0]
    own_slot = tile_slot[0]
    offsets = slot_offset[:, 0, :]
    hits = own_slot[None, :] == jnp.arange(slots, dtype=jnp.int32)[:, None]
    which = jnp.min(jnp.where(hits, jnp.arange(count, dtype=jnp.int32)[None, :], count), axis=1)
    own_matched = match_all(own_tiles, own_coeffs, basis)
    extra = 16
    weight_rows = jnp.broadcast_to(own_weight[:, None, None], (count, extra, size))
    carry = jnp.concatenate([own_matched, weight_rows], axis=1)
    carry = jnp.concatenate([carry, jnp.zeros((1, size + extra, size), jnp.bfloat16)], axis=0)
    send = carry[which].reshape(columns, CAP, size + extra, size)
    filters = detect_filters(patch)
    recv = lax.all_to_all(send, "skyx", split_axis=0, concat_axis=0, tiled=True)
    recv, offsets, filters = lax.optimization_barrier((recv, offsets, filters))
    recv = recv.reshape(slots, size + extra, size)
    matched = recv[:, :size, :]
    recv_weight = recv[:, size, 0]
    coadd = coadd_patch(matched, recv_weight, offsets, patch)
    detection = detect(coadd, *filters)
    return (coadd, detection)


def solution(mesh):
    in_specs = (
        P("skyy", "skyx", None, None),
        P("skyy", "skyx", None, None, None),
        P("skyy", "skyx"),
        P("skyy", "skyx"),
        P(None, "skyy", "skyx"),
    )
    out_specs = (P("skyy", "skyx"), P("skyy", "skyx"))
    return jax.shard_map(body, mesh=mesh, in_specs=in_specs, out_specs=out_specs, check_vma=False)
```
